256 devices in a mesh: seq: 32 (over z, y_lo, core), head: 8 (over x, y_hi).
Axes of the slice: x: 4, y: 4 (y_hi: 2, y_lo: 2; y = y_hi * 2 + y_lo), z: 8, core: 2. Of those that a mesh axis runs over, the one named last changes fastest.
Arguments:
- queries: bfloat16 [32768, 1024], P('seq', 'head'), may hold values from -6 to 6
- keys: bfloat16 [32768, 1024], P('seq', 'head'), may hold values from -6 to 6
- values: bfloat16 [32768, 1024], P('seq', 'head'), may hold values from -6 to 6
- gates: bfloat16 [32768, 1024], P('seq', 'head'), may hold values from -6 to 6
- sessions: int32 [32768], P('seq'), may hold values from 0 to 15, never falling along the last dimension, each value on 1 to 3072 neighbouring positions
- score_bias: float32 [8], P('head'), may hold values from -1 to 1
- grad_out: bfloat16 [32768, 1024], P('seq', 'head'), may hold values from -6 to 6
- w_out: bfloat16 [1024, 1024], P('head'), may hold values from -0.1875 to 0.1875
Outputs:
- grad_queries: float32 [32768, 1024], P('seq', 'head')
- grad_keys: float32 [32768, 1024], P('seq', 'head')
- grad_values: float32 [32768, 1024], P('seq', 'head')
- grad_gates: float32 [32768, 1024], P('seq', 'head')
- grad_w_out: float32 [1024, 1024], P('head', 'seq')
The draws below stay inside these ranges and needn't reach their ends.
Inputs may be any that keep to these rules, and one draw needn't show every extreme that they name: `sessions`: session numbers never fall from one event to the next; every session number is used, each session has 1 to 3072 events and one has exactly 3072.
All inputs are finite; a program needn't handle non-finite values.
Results may differ from the reference program's by a relative error of at most 0.0042.
Values may be sent and summed in bfloat16 or wider, within the bound.
No kernel may reach another device: no remote copies, remote signals or barrier semaphores. Data moves between devices by JAX's collectives and lax.ppermute only.
A program may use at most 128 MiB of HBM per device.

```python
import math
import jax
import jax.numpy as jnp
import numpy as np
from jax import lax

H = 8
DH = 128
D = 1024
TOK_DEV = 1024
TOKENS = 32768
SESS_MAX = 3072
SESSIONS = 16


def raised(entries, rng, source, target, shards_of, factor):
    def block_of(position):
        return (jnp.arange(entries.shape[position]) // (entries.shape[position] // shards_of)).reshape((-1,) + (1,) * (entries.ndim - 1 - position))

    one_side = jax.random.permutation(rng, shards_of)[block_of(target)]
    second = (block_of(target) + shards_of // 2) % shards_of
    return jnp.where((block_of(source) == one_side) | (block_of(source) == second), factor * entries, entries)


def block_levels(rng, shape, pieces, least, largest):
    gain, own = 1.0, jax.random.fold_in(rng, 6)
    for position, blocks in pieces:
        draws = jnp.exp(jax.random.uniform(jax.random.fold_in(own, position), (blocks,), jnp.float32, least / len(pieces), largest / len(pieces)))
        gain = gain * jnp.repeat(draws, shape[position] // blocks).reshape([-1 if axis == position else 1 for axis in range(len(shape))])
    return gain


def split_up(count, total, bound, lean):
    portions = [(1 << 20) // math.isqrt(rank ** lean) + 1 for rank in range(2, count + 1)]
    surplus, holding = total - bound - (count - 1), [1] * (count - 1)
    while surplus > 0:
        candidates = [i for i in range(count - 1) if holding[i] < bound]
        mass, budget = sum([portions[i] for i in candidates]), surplus
        for i in candidates:
            more = min(bound - holding[i], max(1, budget * portions[i] // mass), surplus)
            holding[i] = holding[i] + more
            surplus = surplus - more
    return np.array([bound] + holding)


def uneven_parts(rng, amount, total, most, lean):
    if amount == 2:
        one = jax.random.randint(rng, (), max(1, total - most), min(most, total - 1) + 1)
        return jnp.stack([one, total - one])
    sizes = jnp.asarray(split_up(amount, total, most, lean), jnp.int32)
    twos = (amount - 1) // 2
    giver, taker = sizes[1:1 + 2 * twos:2], sizes[2:2 + 2 * twos:2]
    slack = jnp.minimum(giver - 1, most - taker)
    shifted = jax.random.randint(jax.random.fold_in(rng, 1), (twos,), 0, 1 << 20) % (slack + 1)
    sizes = sizes.at[1:1 + 2 * twos:2].set(giver - shifted).at[2:2 + 2 * twos:2].set(taker + shifted)
    return sizes[jax.random.permutation(jax.random.fold_in(rng, 2), amount)]


def noise(own_key, dims, width, bound, cuts=(), held_as=jnp.bfloat16):
    loudness = block_levels(own_key, dims, cuts, -0.22, 0.18) if cuts else 1.0
    array = jax.random.normal(own_key, dims, jnp.float32) * width * loudness
    return jnp.minimum(jnp.maximum(array, -bound), bound).astype(held_as)


def noise_with(stream_key, extent, deviation, bound, split, heavy, kind=jnp.bfloat16):
    entries = deviation * jax.random.normal(stream_key, extent, jnp.float32)
    if split:
        entries = entries * block_levels(stream_key, extent, split, -0.22, 0.18)
    return jnp.clip(raised(entries, jax.random.fold_in(stream_key, 3), *heavy), -bound, bound).astype(kind)


def setup_inputs(seed: int = 0) -> dict:
    key_of = jax.random.split(jax.random.key(seed), 9)
    return {
        "queries": noise(key_of[0], (TOKENS, D), 1.0, 6.0, ((0, 32), (1, 8))),
        "keys": noise(key_of[1], (TOKENS, D), 1.0, 6.0, ((0, 32), (1, 8))),
        "values": noise(key_of[2], (TOKENS, D), 1.0, 6.0, ((0, 32), (1, 8))),
        "gates": noise(key_of[3], (TOKENS, D), 1.0, 6.0, ((0, 32), (1, 8))),
        "sessions": jnp.searchsorted(jnp.cumsum(uneven_parts(key_of[4], SESSIONS, TOKENS, SESS_MAX, 2)), jnp.arange(TOKENS), side="right").astype(jnp.int32),
        "score_bias": jnp.clip(jax.random.uniform(key_of[5], (H,), jnp.float32, -1.0, 1.0) * block_levels(key_of[5], (H,), ((0, 8),), -0.4, 0.0), -1.0, 1.0),
        "grad_out": noise_with(key_of[6], (TOKENS, D), 1.0, 6.0, ((0, 32), (1, 8)), (0, 1, 32, 2.75)),
        "w_out": noise(key_of[7], (D, D), D ** -0.5, 0.1875, ((0, 8),)),
    }


def silu_parts(scores):
    sigma = jax.nn.sigmoid(scores)
    return (scores * sigma, sigma * (1.0 + scores * (1.0 - sigma)))

def reference(queries, keys, values, gates, sessions, score_bias, grad_out, w_out):
    event_count = queries.shape[0]
    back_rows = 3 * TOK_DEV
    scale = 1.0 / math.sqrt(DH)
    block_count = event_count // TOK_DEV
    q_heads = queries.astype(jnp.float32).reshape(event_count, H, DH)
    k_heads = keys.astype(jnp.float32).reshape(event_count, H, DH)
    v_heads = values.astype(jnp.float32).reshape(event_count, H, DH)
    pad_rows = jnp.zeros((back_rows, H, DH), jnp.float32)
    keys_padded = jnp.concatenate([pad_rows, k_heads], 0)
    values_padded = jnp.concatenate([pad_rows, v_heads], 0)
    sessions_padded = jnp.concatenate([jnp.full((back_rows,), -1, jnp.int32), sessions.astype(jnp.int32)], 0)
    bias_col = score_bias.astype(jnp.float32).reshape(H, 1, 1)
    local_pos = jnp.arange(TOK_DEV, dtype=jnp.int32)
    window_pos = jnp.arange(4 * TOK_DEV, dtype=jnp.int32) - back_rows

    def block_setup(block_index):
        first_row = (block_index * TOK_DEV).astype(jnp.int32)
        q_block = lax.dynamic_slice_in_dim(q_heads, first_row, TOK_DEV, 0)
        k_block = lax.dynamic_slice_in_dim(keys_padded, first_row, 4 * TOK_DEV, 0)
        v_block = lax.dynamic_slice_in_dim(values_padded, first_row, 4 * TOK_DEV, 0)
        key_sessions = lax.dynamic_slice_in_dim(sessions_padded, first_row, 4 * TOK_DEV, 0)
        query_sessions = lax.dynamic_slice_in_dim(sessions.astype(jnp.int32), first_row, TOK_DEV, 0)
        allowed = (query_sessions[:, None] == key_sessions[None, :]) & (window_pos[None, :] <= local_pos[:, None])
        scores = jnp.einsum('ihd,jhd->hij', q_block, k_block, precision=lax.Precision.HIGHEST) * scale + bias_col
        return (first_row, q_block, k_block, v_block, allowed, scores)

    def forward_block(block_index):
        first_row, q_block, k_block, v_block, allowed, scores = block_setup(block_index)
        act, deriv = silu_parts(scores)
        weights = jnp.where(allowed[None], act, 0.0).astype(jnp.bfloat16).astype(jnp.float32)
        return jnp.einsum('hij,jhd->ihd', weights, v_block, precision=lax.Precision.HIGHEST)
    block_ids = jnp.arange(block_count, dtype=jnp.int32)
    attended = lax.map(forward_block, block_ids).reshape(event_count, H, DH)
    centered = attended - lax.optimization_barrier(jnp.mean(attended, axis=-1, keepdims=True))
    inv_std = lax.rsqrt(lax.optimization_barrier(jnp.mean(centered * centered, axis=-1, keepdims=True)) + 1e-05)
    normed = centered * inv_std
    gate_heads = gates.astype(jnp.float32).reshape(event_count, H, DH)
    mixed = (normed * gate_heads).astype(jnp.bfloat16).reshape(event_count, H * DH)
    grad_mixed = jnp.dot(grad_out, w_out.T, preferred_element_type=jnp.float32).reshape(event_count, H, DH)
    grad_gates = (grad_mixed * normed).reshape(event_count, H * DH)
    grad_normed = grad_mixed * gate_heads
    grad_attended = (grad_normed - lax.optimization_barrier(jnp.mean(grad_normed, axis=-1, keepdims=True)) - normed * lax.optimization_barrier(jnp.mean(grad_normed * normed, axis=-1, keepdims=True))) * inv_std
    grad_attended = grad_attended.astype(jnp.bfloat16).astype(jnp.float32)

    def backward_block(accum, block_index):
        grad_keys_pad, grad_values_pad = accum
        first_row, q_block, k_block, v_block, allowed, scores = block_setup(block_index)
        act, deriv = silu_parts(scores)
        weights = jnp.where(allowed[None], act, 0.0).astype(jnp.bfloat16).astype(jnp.float32)
        grad_block = lax.dynamic_slice_in_dim(grad_attended, first_row, TOK_DEV, 0)
        values_term = jnp.einsum('hij,ihd->jhd', weights, grad_block, precision=lax.Precision.HIGHEST)
        grad_weights = jnp.einsum('ihd,jhd->hij', grad_block, v_block, precision=lax.Precision.HIGHEST)
        grad_scores = jnp.where(allowed[None], grad_weights * deriv * scale, 0.0).astype(jnp.bfloat16).astype(jnp.float32)
        query_term = jnp.einsum('hij,jhd->ihd', grad_scores, k_block, precision=lax.Precision.HIGHEST)
        keys_term = jnp.einsum('hij,ihd->jhd', grad_scores, q_block, precision=lax.Precision.HIGHEST)
        old_keys = lax.dynamic_slice_in_dim(grad_keys_pad, first_row, 4 * TOK_DEV, 0)
        old_values = lax.dynamic_slice_in_dim(grad_values_pad, first_row, 4 * TOK_DEV, 0)
        grad_keys_pad = lax.dynamic_update_slice_in_dim(grad_keys_pad, old_keys + keys_term, first_row, 0)
        grad_values_pad = lax.dynamic_update_slice_in_dim(grad_values_pad, old_values + values_term, first_row, 0)
        return ((grad_keys_pad, grad_values_pad), query_term)
    start_accum = (jnp.zeros((event_count + back_rows, H, DH), jnp.float32), jnp.zeros((event_count + back_rows, H, DH), jnp.float32))
    (grad_keys_pad, grad_values_pad), query_terms = lax.scan(backward_block, start_accum, block_ids)
    grad_queries = query_terms.reshape(event_count, H * DH)
    grad_keys = grad_keys_pad[back_rows:].reshape(event_count, H * DH)
    grad_values = grad_values_pad[back_rows:].reshape(event_count, H * DH)
    grad_w_out = jnp.dot(mixed.T, grad_out, preferred_element_type=jnp.float32)
    return (grad_queries, grad_keys, grad_values, grad_gates, grad_w_out)
```

```python
import math

import jax
import jax.numpy as jnp
from jax import lax
from jax.sharding import PartitionSpec as P

DH = 128


back_steps = (1, 2, 3)
norm_eps = 1e-05


def shifted(block, axis, distance):
    devices = range(lax.axis_size(axis))
    route = [(i - distance, i) for i in devices if i - distance in devices]
    return lax.ppermute(block, axis, route)


def halving_scatter(block, axis):
    count = lax.axis_size(axis)
    my_index = lax.axis_index(axis)
    rows, cols = block.shape
    levels = count.bit_length() - 1
    current = block.reshape((rows,) + (2,) * levels + (cols // count,))
    for level in range(levels):
        bit = 1 << level
        axis_pos = current.ndim - 2
        mine = (my_index // bit) % 2
        low = lax.index_in_dim(current, 0, axis_pos, keepdims=False)
        high = lax.index_in_dim(current, 1, axis_pos, keepdims=False)
        keep = jnp.where(mine == 0, low, high)
        send = jnp.where(mine == 0, high, low)
        current = keep + lax.ppermute(send, axis, [(i, i ^ bit) for i in range(count)])
    return current.reshape(rows, cols // count)


def silu_parts(scores):
    sigma = jax.nn.sigmoid(scores)
    return (scores * sigma, sigma * (1.0 + scores * (1.0 - sigma)))


def per_device(queries, keys, values, gates, sessions, score_bias, grad_out, w_out):
    row_count = queries.shape[0]
    feature_count = queries.shape[1]
    head_count = feature_count // DH
    scale = 1.0 / math.sqrt(DH)
    my_index = lax.axis_index("seq")
    q_heads = queries.reshape(row_count, head_count, DH)
    bias_col = score_bias.reshape(head_count, 1, 1)
    offsets = jnp.arange(row_count, dtype=jnp.int32)
    packed = jnp.stack([keys, values])
    windows = [(packed, sessions)]
    for distance in back_steps:
        windows.append(shifted((packed, sessions), "seq", distance))
    prepared = []
    for distance in range(4):
        key_pack, key_sessions = windows[distance]
        allowed = (sessions[:, None] == key_sessions[None, :]) & (my_index >= distance)
        if distance == 0:
            allowed = allowed & (offsets[None, :] <= offsets[:, None])
        k_heads = key_pack[0].reshape(row_count, head_count, DH)
        v_heads = key_pack[1].reshape(row_count, head_count, DH)
        prepared.append((k_heads, v_heads, allowed))

    def pair_scores(query_heads, k_heads):
        raw = jnp.einsum("ihd,jhd->hij", query_heads, k_heads, preferred_element_type=jnp.float32)
        return raw * scale + bias_col

    attended = jnp.zeros((row_count, head_count, DH), jnp.float32)
    for k_heads, v_heads, allowed in prepared:
        act, deriv = silu_parts(pair_scores(q_heads, k_heads))
        weights = jnp.where(allowed[None], act, 0.0).astype(jnp.bfloat16)
        attended = attended + jnp.einsum(
            "hij,jhd->ihd", weights, v_heads, preferred_element_type=jnp.float32
        )
    centered = attended - jnp.mean(attended, axis=-1, keepdims=True)
    inv_std = lax.rsqrt(jnp.mean(centered * centered, axis=-1, keepdims=True) + norm_eps)
    normed = centered * inv_std
    gate_heads = gates.reshape(row_count, head_count, DH).astype(jnp.float32)
    mixed = (normed * gate_heads).astype(jnp.bfloat16).reshape(row_count, feature_count)
    head_devices = lax.axis_size("head")
    head_index = lax.axis_index("head")
    gathered_blocks = [grad_out] + [
        lax.ppermute(grad_out, "head", [(i, (i + k) % head_devices) for i in range(head_devices)])
        for k in range(1, head_devices)
    ]
    column_block = jnp.concatenate(gathered_blocks, axis=1)
    block_width = grad_out.shape[1]
    source_block = (head_index - jnp.arange(head_devices)) % head_devices
    w_blocks = w_out.reshape(w_out.shape[0], head_devices, block_width)
    w_in_order = jnp.take(w_blocks, source_block, axis=1).reshape(w_out.shape)
    grad_mixed = lax.dot_general(
        column_block, w_in_order, (((1,), (1,)), ((), ())), preferred_element_type=jnp.float32
    )
    product = lax.dot_general(
        mixed, column_block, (((0,), (0,)), ((), ())), preferred_element_type=jnp.float32
    )
    gather_back = (head_index - jnp.arange(head_devices)) % head_devices
    weight_rows = jnp.take(
        product.reshape(product.shape[0], head_devices, block_width), gather_back, axis=1
    ).reshape(product.shape)
    grad_w_out = halving_scatter(weight_rows, "seq")
    grad_mixed = grad_mixed.reshape(row_count, head_count, DH)
    grad_gates = (grad_mixed * normed).reshape(row_count, feature_count)
    grad_normed = grad_mixed * gate_heads
    grad_attended = (
        grad_normed
        - jnp.mean(grad_normed, axis=-1, keepdims=True)
        - normed * jnp.mean(grad_normed * normed, axis=-1, keepdims=True)
    ) * inv_std
    grad_attended = grad_attended.astype(jnp.bfloat16)
    grad_queries = jnp.zeros((row_count, head_count, DH), jnp.float32)
    key_terms = []
    for window_index in range(4):
        k_heads, v_heads, allowed = prepared[window_index]
        scores = pair_scores(q_heads, k_heads)
        key_act, key_deriv = silu_parts(scores)
        key_weights = jnp.where(allowed[None], key_act, 0.0).astype(jnp.bfloat16)
        values_term = jnp.einsum(
            "hij,ihd->jhd", key_weights, grad_attended, preferred_element_type=jnp.float32
        )
        grad_weights = jnp.einsum(
            "ihd,jhd->hij", grad_attended, v_heads, preferred_element_type=jnp.float32
        )
        grad_scores = jnp.where(allowed[None], grad_weights * key_deriv * scale, 0.0).astype(
            jnp.bfloat16
        )
        keys_term = jnp.einsum(
            "hij,ihd->jhd", grad_scores, q_heads, preferred_element_type=jnp.float32
        )
        grad_scores, term_pair = (
            grad_scores,
            jnp.stack(
                [
                    keys_term.reshape(row_count, feature_count),
                    values_term.reshape(row_count, feature_count),
                ]
            ),
        )
        key_terms.append(term_pair)
        grad_queries = grad_queries + jnp.einsum(
            "hij,jhd->ihd", grad_scores, k_heads, preferred_element_type=jnp.float32
        )
    summed = key_terms[0]
    for distance in back_steps:
        summed = summed + shifted(key_terms[distance], "seq", -distance)
    return (
        grad_queries.reshape(row_count, feature_count),
        summed[0],
        summed[1],
        grad_gates,
        grad_w_out,
    )


def solution(mesh):
    return jax.shard_map(
        per_device,
        mesh=mesh,
        in_specs=(
            P("seq", "head"),
            P("seq", "head"),
            P("seq", "head"),
            P("seq", "head"),
            P("seq"),
            P("head"),
            P("seq", "head"),
            P("head", None),
        ),
        out_specs=(
            P("seq", "head"),
            P("seq", "head"),
            P("seq", "head"),
            P("seq", "head"),
            P("head", "seq"),
        ),
        check_vma=False,
    )
```

```python
import math

import jax
import jax.numpy as jnp
from jax import lax
from jax.sharding import PartitionSpec as P

DH = 128


back_steps = (1, 2, 3)
norm_eps = 1e-05


def shifted(block, axis, distance):
    devices = range(lax.axis_size(axis))
    route = [(i - distance, i) for i in devices if i - distance in devices]
    return lax.ppermute(block, axis, route)


def halving_scatter(block, axis):
    count = lax.axis_size(axis)
    my_index = lax.axis_index(axis)
    rows, cols = block.shape
    levels = count.bit_length() - 1
    current = block.reshape((rows,) + (2,) * levels + (cols // count,))
    for level in range(levels):
        bit = 1 << level
        axis_pos = current.ndim - 2
        mine = (my_index // bit) % 2
        low = lax.index_in_dim(current, 0, axis_pos, keepdims=False)
        high = lax.index_in_dim(current, 1, axis_pos, keepdims=False)
        keep = jnp.where(mine == 0, low, high)
        send = jnp.where(mine == 0, high, low)
        current = keep + lax.ppermute(send, axis, [(i, i ^ bit) for i in range(count)])
    return current.reshape(rows, cols // count)


def silu_parts(scores):
    sigma = jax.nn.sigmoid(scores)
    return (scores * sigma, sigma * (1.0 + scores * (1.0 - sigma)))


def per_device(queries, keys, values, gates, sessions, score_bias, grad_out, w_out):
    row_count = queries.shape[0]
    feature_count = queries.shape[1]
    head_count = feature_count // DH
    scale = 1.0 / math.sqrt(DH)
    seq_devices = lax.axis_size("seq")
    my_index = lax.axis_index("seq")
    bias_col = score_bias.reshape(head_count, 1, 1)
    offsets = jnp.arange(row_count, dtype=jnp.int32)

    def heads_of(block):
        return block.reshape(row_count, head_count, DH)

    session_rows = sessions.astype(jnp.bfloat16).reshape(-1, feature_count)
    kv_pack = jnp.concatenate([keys, values, session_rows], axis=0)
    q_pack = jnp.concatenate([queries, session_rows], axis=0)

    def sessions_of(pack, start):
        return pack[start:].reshape(-1)[:row_count].astype(jnp.int32)

    kv_from = {d: shifted(kv_pack, "seq", d) for d in back_steps}
    q_from = {d: shifted(q_pack, "seq", -d) for d in back_steps}

    head_devices = lax.axis_size("head")
    head_index = lax.axis_index("head")
    gathered_blocks = [grad_out] + [
        lax.ppermute(grad_out, "head", [(i, (i + k) % head_devices) for i in range(head_devices)])
        for k in range(1, head_devices)
    ]

    q_heads = heads_of(queries)
    k_own = heads_of(keys)
    v_own = heads_of(values)

    def pair_scores(query_heads, k_heads):
        raw = jnp.einsum("ihd,jhd->hij", query_heads, k_heads, preferred_element_type=jnp.float32)
        return raw * scale + bias_col

    prepared = []
    for distance in range(4):
        if distance == 0:
            k_heads, v_heads, key_sessions = k_own, v_own, sessions
            allowed = (sessions[:, None] == key_sessions[None, :]) & (
                offsets[None, :] <= offsets[:, None]
            )
        else:
            pack = kv_from[distance]
            k_heads = heads_of(pack[:row_count])
            v_heads = heads_of(pack[row_count : 2 * row_count])
            key_sessions = sessions_of(pack, 2 * row_count)
            allowed = (sessions[:, None] == key_sessions[None, :]) & (my_index >= distance)
        prepared.append((k_heads, v_heads, allowed))

    attended = jnp.zeros((row_count, head_count, DH), jnp.float32)
    for k_heads, v_heads, allowed in prepared:
        act, deriv = silu_parts(pair_scores(q_heads, k_heads))
        weights = jnp.where(allowed[None], act, 0.0).astype(jnp.bfloat16)
        attended = attended + jnp.einsum(
            "hij,jhd->ihd", weights, v_heads, preferred_element_type=jnp.float32
        )
    centered = attended - jnp.mean(attended, axis=-1, keepdims=True)
    inv_std = lax.rsqrt(jnp.mean(centered * centered, axis=-1, keepdims=True) + norm_eps)
    normed = centered * inv_std
    gate_heads = gates.reshape(row_count, head_count, DH).astype(jnp.float32)
    mixed = (normed * gate_heads).astype(jnp.bfloat16).reshape(row_count, feature_count)

    column_block = jnp.concatenate(gathered_blocks, axis=1)
    block_width = grad_out.shape[1]
    source_block = (head_index - jnp.arange(head_devices)) % head_devices
    w_blocks = w_out.reshape(w_out.shape[0], head_devices, block_width)
    w_in_order = jnp.take(w_blocks, source_block, axis=1).reshape(w_out.shape)
    grad_mixed = lax.dot_general(
        column_block, w_in_order, (((1,), (1,)), ((), ())), preferred_element_type=jnp.float32
    )
    product = lax.dot_general(
        mixed, column_block, (((0,), (0,)), ((), ())), preferred_element_type=jnp.float32
    )
    weight_rows = jnp.take(
        product.reshape(product.shape[0], head_devices, block_width), source_block, axis=1
    ).reshape(product.shape)
    grad_w_out = halving_scatter(weight_rows, "seq")

    grad_mixed = grad_mixed.reshape(row_count, head_count, DH)
    grad_gates = (grad_mixed * normed).reshape(row_count, feature_count)
    grad_normed = grad_mixed * gate_heads
    grad_attended = (
        grad_normed
        - jnp.mean(grad_normed, axis=-1, keepdims=True)
        - normed * jnp.mean(grad_normed * normed, axis=-1, keepdims=True)
    ) * inv_std
    grad_attended = grad_attended.astype(jnp.bfloat16)
    grad_attended_from = {
        d: heads_of(shifted(grad_attended.reshape(row_count, feature_count), "seq", -d))
        for d in back_steps
    }

    grad_queries = jnp.zeros((row_count, head_count, DH), jnp.float32)
    for k_heads, v_heads, allowed in prepared:
        scores = pair_scores(q_heads, k_heads)
        _, deriv = silu_parts(scores)
        grad_weights = jnp.einsum(
            "ihd,jhd->hij", grad_attended, v_heads, preferred_element_type=jnp.float32
        )
        grad_scores = jnp.where(allowed[None], grad_weights * deriv * scale, 0.0).astype(
            jnp.bfloat16
        )
        grad_queries = grad_queries + jnp.einsum(
            "hij,jhd->ihd", grad_scores, k_heads, preferred_element_type=jnp.float32
        )

    key_windows = [(q_heads, sessions, grad_attended, prepared[0][2])]
    for distance in back_steps:
        pack = q_from[distance]
        query_sessions = sessions_of(pack, row_count)
        allowed = (query_sessions[:, None] == sessions[None, :]) & (
            my_index + distance < seq_devices
        )
        key_windows.append(
            (heads_of(pack[:row_count]), query_sessions, grad_attended_from[distance], allowed)
        )
    grad_keys = jnp.zeros((row_count, head_count, DH), jnp.float32)
    grad_values = jnp.zeros((row_count, head_count, DH), jnp.float32)
    for query_heads, _, grad_block, allowed in key_windows:
        scores = pair_scores(query_heads, k_own)
        act, deriv = silu_parts(scores)
        weights = jnp.where(allowed[None], act, 0.0).astype(jnp.bfloat16)
        grad_values = grad_values + jnp.einsum(
            "hij,ihd->jhd", weights, grad_block, preferred_element_type=jnp.float32
        )
        grad_weights = jnp.einsum(
            "ihd,jhd->hij", grad_block, v_own, preferred_element_type=jnp.float32
        )
        grad_scores = jnp.where(allowed[None], grad_weights * deriv * scale, 0.0).astype(
            jnp.bfloat16
        )
        grad_keys = grad_keys + jnp.einsum(
            "hij,ihd->jhd", grad_scores, query_heads, preferred_element_type=jnp.float32
        )
    return (
        grad_queries.reshape(row_count, feature_count),
        grad_keys.reshape(row_count, feature_count),
        grad_values.reshape(row_count, feature_count),
        grad_gates,
        grad_w_out,
    )


def solution(mesh):
    return jax.shard_map(
        per_device,
        mesh=mesh,
        in_specs=(
            P("seq", "head"),
            P("seq", "head"),
            P("seq", "head"),
            P("seq", "head"),
            P("seq"),
            P("head"),
            P("seq", "head"),
            P("head", None),
        ),
        out_specs=(
            P("seq", "head"),
            P("seq", "head"),
            P("seq", "head"),
            P("seq", "head"),
            P("head", "seq"),
        ),
        check_vma=False,
    )
```

```python
import math

import jax
import jax.numpy as jnp
from jax import lax
from jax.sharding import PartitionSpec as P

DH = 128


back_steps = (1, 2, 3)
norm_eps = 1e-05


def shifted(block, axis, distance):
    devices = range(lax.axis_size(axis))
    route = [(i - distance, i) for i in devices if i - distance in devices]
    return lax.ppermute(block, axis, route)


def halving_scatter(block, axis):
    count = lax.axis_size(axis)
    my_index = lax.axis_index(axis)
    rows, cols = block.shape
    levels = count.bit_length() - 1
    current = block.reshape((rows,) + (2,) * levels + (cols // count,))
    for level in range(levels):
        bit = 1 << level
        axis_pos = current.ndim - 2
        mine = (my_index // bit) % 2
        low = lax.index_in_dim(current, 0, axis_pos, keepdims=False)
        high = lax.index_in_dim(current, 1, axis_pos, keepdims=False)
        keep = jnp.where(mine == 0, low, high)
        send = jnp.where(mine == 0, high, low)
        current = keep + lax.ppermute(send, axis, [(i, i ^ bit) for i in range(count)])
    return current.reshape(rows, cols // count)


def silu_parts(scores):
    sigma = jax.nn.sigmoid(scores)
    return (scores * sigma, sigma * (1.0 + scores * (1.0 - sigma)))


def per_device(queries, keys, values, gates, sessions, score_bias, grad_out, w_out):
    row_count = queries.shape[0]
    feature_count = queries.shape[1]
    head_count = feature_count // DH
    scale = 1.0 / math.sqrt(DH)
    my_index = lax.axis_index("seq")
    q_heads = queries.reshape(row_count, head_count, DH)
    bias_col = score_bias.reshape(head_count, 1, 1)
    offsets = jnp.arange(row_count, dtype=jnp.int32)
    session_rows = sessions.astype(jnp.bfloat16).reshape(-1, feature_count)
    packed = jnp.concatenate([keys, values, session_rows], axis=0)
    windows = [packed]
    for distance in back_steps:
        windows.append(shifted(packed, "seq", distance))
    prepared = []
    for distance in range(4):
        key_pack = windows[distance]
        if distance == 0:
            key_sessions = sessions
        else:
            key_sessions = key_pack[2 * row_count :].reshape(-1)[:row_count].astype(jnp.int32)
        allowed = (sessions[:, None] == key_sessions[None, :]) & (my_index >= distance)
        if distance == 0:
            allowed = allowed & (offsets[None, :] <= offsets[:, None])
        k_heads = key_pack[:row_count].reshape(row_count, head_count, DH)
        v_heads = key_pack[row_count : 2 * row_count].reshape(row_count, head_count, DH)
        prepared.append((k_heads, v_heads, allowed))

    def pair_scores(query_heads, k_heads):
        raw = jnp.einsum("ihd,jhd->hij", query_heads, k_heads, preferred_element_type=jnp.float32)
        return raw * scale + bias_col

    attended = jnp.zeros((row_count, head_count, DH), jnp.float32)
    for k_heads, v_heads, allowed in prepared:
        act, deriv = silu_parts(pair_scores(q_heads, k_heads))
        weights = jnp.where(allowed[None], act, 0.0).astype(jnp.bfloat16)
        attended = attended + jnp.einsum(
            "hij,jhd->ihd", weights, v_heads, preferred_element_type=jnp.float32
        )
    centered = attended - jnp.mean(attended, axis=-1, keepdims=True)
    inv_std = lax.rsqrt(jnp.mean(centered * centered, axis=-1, keepdims=True) + norm_eps)
    normed = centered * inv_std
    gate_heads = gates.reshape(row_count, head_count, DH).astype(jnp.float32)
    mixed = (normed * gate_heads).astype(jnp.bfloat16).reshape(row_count, feature_count)
    head_devices = lax.axis_size("head")
    head_index = lax.axis_index("head")
    gathered_blocks = [grad_out] + [
        lax.ppermute(grad_out, "head", [(i, (i + k) % head_devices) for i in range(head_devices)])
        for k in range(1, head_devices)
    ]
    column_block = jnp.concatenate(gathered_blocks, axis=1)
    block_width = grad_out.shape[1]
    source_block = (head_index - jnp.arange(head_devices)) % head_devices
    w_blocks = w_out.reshape(w_out.shape[0], head_devices, block_width)
    w_in_order = jnp.take(w_blocks, source_block, axis=1).reshape(w_out.shape)
    grad_mixed = lax.dot_general(
        column_block, w_in_order, (((1,), (1,)), ((), ())), preferred_element_type=jnp.float32
    )
    product = lax.dot_general(
        mixed, column_block, (((0,), (0,)), ((), ())), preferred_element_type=jnp.float32
    )
    gather_back = (head_index - jnp.arange(head_devices)) % head_devices
    weight_rows = jnp.take(
        product.reshape(product.shape[0], head_devices, block_width), gather_back, axis=1
    ).reshape(product.shape)
    grad_w_out = halving_scatter(weight_rows, "seq")
    grad_mixed = grad_mixed.reshape(row_count, head_count, DH)
    grad_gates = (grad_mixed * normed).reshape(row_count, feature_count)
    grad_normed = grad_mixed * gate_heads
    grad_attended = (
        grad_normed
        - jnp.mean(grad_normed, axis=-1, keepdims=True)
        - normed * jnp.mean(grad_normed * normed, axis=-1, keepdims=True)
    ) * inv_std
    grad_attended = grad_attended.astype(jnp.bfloat16)
    grad_queries = jnp.zeros((row_count, head_count, DH), jnp.float32)
    key_terms = []
    for window_index in range(4):
        k_heads, v_heads, allowed = prepared[window_index]
        scores = pair_scores(q_heads, k_heads)
        key_act, key_deriv = silu_parts(scores)
        key_weights = jnp.where(allowed[None], key_act, 0.0).astype(jnp.bfloat16)
        values_term = jnp.einsum(
            "hij,ihd->jhd", key_weights, grad_attended, preferred_element_type=jnp.float32
        )
        grad_weights = jnp.einsum(
            "ihd,jhd->hij", grad_attended, v_heads, preferred_element_type=jnp.float32
        )
        grad_scores = jnp.where(allowed[None], grad_weights * key_deriv * scale, 0.0).astype(
            jnp.bfloat16
        )
        keys_term = jnp.einsum(
            "hij,ihd->jhd", grad_scores, q_heads, preferred_element_type=jnp.float32
        )
        grad_scores, term_pair = (
            grad_scores,
            jnp.stack(
                [
                    keys_term.reshape(row_count, feature_count),
                    values_term.reshape(row_count, feature_count),
                ]
            ),
        )
        key_terms.append(term_pair)
        grad_queries = grad_queries + jnp.einsum(
            "hij,jhd->ihd", grad_scores, k_heads, preferred_element_type=jnp.float32
        )
    summed = key_terms[0]
    for distance in back_steps:
        sent = shifted(key_terms[distance].astype(jnp.bfloat16), "seq", -distance)
        summed = summed + sent.astype(jnp.float32)
    return (
        grad_queries.reshape(row_count, feature_count),
        summed[0],
        summed[1],
        grad_gates,
        grad_w_out,
    )


def solution(mesh):
    return jax.shard_map(
        per_device,
        mesh=mesh,
        in_specs=(
            P("seq", "head"),
            P("seq", "head"),
            P("seq", "head"),
            P("seq", "head"),
            P("seq"),
            P("head"),
            P("seq", "head"),
            P("head", None),
        ),
        out_specs=(
            P("seq", "head"),
            P("seq", "head"),
            P("seq", "head"),
            P("seq", "head"),
            P("head", "seq"),
        ),
        check_vma=False,
    )
```

```python
import math

import jax
import jax.numpy as jnp
from jax import lax
from jax.sharding import PartitionSpec as P

DH = 128


back_steps = (1, 2, 3)
norm_eps = 1e-05


def shifted(block, axis, distance):
    devices = range(lax.axis_size(axis))
    route = [(i - distance, i) for i in devices if i - distance in devices]
    return lax.ppermute(block, axis, route)


def halving_start(block, axis):
    count = lax.axis_size(axis)
    rows, cols = block.shape
    levels = count.bit_length() - 1
    return block.reshape((rows,) + (2,) * levels + (cols // count,))


def halving_step(current, axis, level):
    count = lax.axis_size(axis)
    my_index = lax.axis_index(axis)
    bit = 1 << level
    axis_pos = current.ndim - 2
    mine = (my_index // bit) % 2
    low = lax.index_in_dim(current, 0, axis_pos, keepdims=False)
    high = lax.index_in_dim(current, 1, axis_pos, keepdims=False)
    keep = jnp.where(mine == 0, low, high)
    send = jnp.where(mine == 0, high, low)
    return keep + lax.ppermute(send, axis, [(i, i ^ bit) for i in range(count)])


def silu_parts(scores):
    sigma = jax.nn.sigmoid(scores)
    return (scores * sigma, sigma * (1.0 + scores * (1.0 - sigma)))


def per_device(queries, keys, values, gates, sessions, score_bias, grad_out, w_out):
    row_count = queries.shape[0]
    feature_count = queries.shape[1]
    head_count = feature_count // DH
    scale = 1.0 / math.sqrt(DH)
    my_index = lax.axis_index("seq")
    q_heads = queries.reshape(row_count, head_count, DH)
    bias_col = score_bias.reshape(head_count, 1, 1)
    offsets = jnp.arange(row_count, dtype=jnp.int32)
    session_rows = sessions.astype(jnp.bfloat16).reshape(-1, feature_count)
    packed = jnp.concatenate([keys, values, session_rows], axis=0)
    windows = [packed]
    for distance in back_steps:
        windows.append(shifted(packed, "seq", distance))
    prepared = []
    for distance in range(4):
        key_pack = windows[distance]
        if distance == 0:
            key_sessions = sessions
        else:
            key_sessions = key_pack[2 * row_count :].reshape(-1)[:row_count].astype(jnp.int32)
        allowed = (sessions[:, None] == key_sessions[None, :]) & (my_index >= distance)
        if distance == 0:
            allowed = allowed & (offsets[None, :] <= offsets[:, None])
        k_heads = key_pack[:row_count].reshape(row_count, head_count, DH)
        v_heads = key_pack[row_count : 2 * row_count].reshape(row_count, head_count, DH)
        prepared.append((k_heads, v_heads, allowed))

    def pair_scores(query_heads, k_heads):
        raw = jnp.einsum("ihd,jhd->hij", query_heads, k_heads, preferred_element_type=jnp.float32)
        return raw * scale + bias_col

    attended = jnp.zeros((row_count, head_count, DH), jnp.float32)
    for k_heads, v_heads, allowed in prepared:
        act, deriv = silu_parts(pair_scores(q_heads, k_heads))
        weights = jnp.where(allowed[None], act, 0.0).astype(jnp.bfloat16)
        attended = attended + jnp.einsum(
            "hij,jhd->ihd", weights, v_heads, preferred_element_type=jnp.float32
        )
    centered = attended - jnp.mean(attended, axis=-1, keepdims=True)
    inv_std = lax.rsqrt(jnp.mean(centered * centered, axis=-1, keepdims=True) + norm_eps)
    normed = centered * inv_std
    gate_heads = gates.reshape(row_count, head_count, DH).astype(jnp.float32)
    mixed = (normed * gate_heads).astype(jnp.bfloat16).reshape(row_count, feature_count)
    head_devices = lax.axis_size("head")
    head_index = lax.axis_index("head")
    gathered_blocks = [grad_out] + [
        lax.ppermute(grad_out, "head", [(i, (i + k) % head_devices) for i in range(head_devices)])
        for k in range(1, head_devices)
    ]
    column_block = jnp.concatenate(gathered_blocks, axis=1)
    block_width = grad_out.shape[1]
    source_block = (head_index - jnp.arange(head_devices)) % head_devices
    w_blocks = w_out.reshape(w_out.shape[0], head_devices, block_width)
    w_in_order = jnp.take(w_blocks, source_block, axis=1).reshape(w_out.shape)
    grad_mixed = lax.dot_general(
        column_block, w_in_order, (((1,), (1,)), ((), ())), preferred_element_type=jnp.float32
    )
    product = lax.dot_general(
        mixed, column_block, (((0,), (0,)), ((), ())), preferred_element_type=jnp.float32
    )
    gather_back = (head_index - jnp.arange(head_devices)) % head_devices
    weight_rows = jnp.take(
        product.reshape(product.shape[0], head_devices, block_width), gather_back, axis=1
    ).reshape(product.shape)
    halving = halving_start(weight_rows, "seq")
    halving_levels = lax.axis_size("seq").bit_length() - 1
    grad_mixed = grad_mixed.reshape(row_count, head_count, DH)
    grad_gates = (grad_mixed * normed).reshape(row_count, feature_count)
    grad_normed = grad_mixed * gate_heads
    grad_attended = (
        grad_normed
        - jnp.mean(grad_normed, axis=-1, keepdims=True)
        - normed * jnp.mean(grad_normed * normed, axis=-1, keepdims=True)
    ) * inv_std
    grad_attended = grad_attended.astype(jnp.bfloat16)
    grad_queries = jnp.zeros((row_count, head_count, DH), jnp.float32)
    key_terms = []
    done_levels = 0
    for window_index in range(4):
        if window_index > 0 and done_levels < halving_levels:
            halving = halving_step(halving, "seq", done_levels)
            done_levels += 1
            halving, grad_attended = lax.optimization_barrier((halving, grad_attended))
        k_heads, v_heads, allowed = prepared[window_index]
        scores = pair_scores(q_heads, k_heads)
        key_act, key_deriv = silu_parts(scores)
        key_weights = jnp.where(allowed[None], key_act, 0.0).astype(jnp.bfloat16)
        values_term = jnp.einsum(
            "hij,ihd->jhd", key_weights, grad_attended, preferred_element_type=jnp.float32
        )
        grad_weights = jnp.einsum(
            "ihd,jhd->hij", grad_attended, v_heads, preferred_element_type=jnp.float32
        )
        grad_scores = jnp.where(allowed[None], grad_weights * key_deriv * scale, 0.0).astype(
            jnp.bfloat16
        )
        keys_term = jnp.einsum(
            "hij,ihd->jhd", grad_scores, q_heads, preferred_element_type=jnp.float32
        )
        grad_scores, term_pair = (
            grad_scores,
            jnp.stack(
                [
                    keys_term.reshape(row_count, feature_count),
                    values_term.reshape(row_count, feature_count),
                ]
            ),
        )
        key_terms.append(term_pair)
        grad_queries = grad_queries + jnp.einsum(
            "hij,jhd->ihd", grad_scores, k_heads, preferred_element_type=jnp.float32
        )
    summed = key_terms[0]
    for distance in back_steps:
        sent = shifted(key_terms[distance].astype(jnp.bfloat16), "seq", -distance)
        summed = summed + sent.astype(jnp.float32)
    while done_levels < halving_levels:
        halving = halving_step(halving, "seq", done_levels)
        done_levels += 1
    grad_w_out = halving.reshape(halving.shape[0], -1)
    return (
        grad_queries.reshape(row_count, feature_count),
        summed[0],
        summed[1],
        grad_gates,
        grad_w_out,
    )


def solution(mesh):
    return jax.shard_map(
        per_device,
        mesh=mesh,
        in_specs=(
            P("seq", "head"),
            P("seq", "head"),
            P("seq", "head"),
            P("seq", "head"),
            P("seq"),
            P("head"),
            P("seq", "head"),
            P("head", None),
        ),
        out_specs=(
            P("seq", "head"),
            P("seq", "head"),
            P("seq", "head"),
            P("seq", "head"),
            P("head", "seq"),
        ),
        check_vma=False,
    )
```

```python
import math

import jax
import jax.numpy as jnp
from jax import lax
from jax.sharding import PartitionSpec as P

DH = 128


back_steps = (1, 2, 3)
norm_eps = 1e-05


def shifted(block, axis, distance):
    devices = range(lax.axis_size(axis))
    route = [(i - distance, i) for i in devices if i - distance in devices]
    return lax.ppermute(block, axis, route)


def halving_start(block, axis):
    count = lax.axis_size(axis)
    rows, cols = block.shape
    levels = count.bit_length() - 1
    return block.reshape((rows,) + (2,) * levels + (cols // count,))


def halving_step(current, axis, level):
    count = lax.axis_size(axis)
    my_index = lax.axis_index(axis)
    bit = 1 << level
    axis_pos = current.ndim - 2
    mine = (my_index // bit) % 2
    low = lax.index_in_dim(current, 0, axis_pos, keepdims=False)
    high = lax.index_in_dim(current, 1, axis_pos, keepdims=False)
    keep = jnp.where(mine == 0, low, high)
    send = jnp.where(mine == 0, high, low)
    return keep + lax.ppermute(send, axis, [(i, i ^ bit) for i in range(count)])


def silu_parts(scores):
    sigma = jax.nn.sigmoid(scores)
    return (scores * sigma, sigma * (1.0 + scores * (1.0 - sigma)))


def per_device(queries, keys, values, gates, sessions, score_bias, grad_out, w_out):
    row_count = queries.shape[0]
    feature_count = queries.shape[1]
    head_count = feature_count // DH
    scale = 1.0 / math.sqrt(DH)
    my_index = lax.axis_index("seq")
    q_heads = queries.reshape(row_count, head_count, DH)
    bias_col = score_bias.reshape(head_count, 1, 1)
    offsets = jnp.arange(row_count, dtype=jnp.int32)
    session_rows = sessions.astype(jnp.bfloat16).reshape(-1, feature_count)
    packed = jnp.concatenate([keys, values, session_rows], axis=0)
    windows = [packed]
    for distance in back_steps:
        windows.append(shifted(packed, "seq", distance))
    prepared = []
    for distance in range(4):
        key_pack = windows[distance]
        if distance == 0:
            key_sessions = sessions
        else:
            key_sessions = key_pack[2 * row_count :].reshape(-1)[:row_count].astype(jnp.int32)
        allowed = (sessions[:, None] == key_sessions[None, :]) & (my_index >= distance)
        if distance == 0:
            allowed = allowed & (offsets[None, :] <= offsets[:, None])
        k_heads = key_pack[:row_count].reshape(row_count, head_count, DH)
        v_heads = key_pack[row_count : 2 * row_count].reshape(row_count, head_count, DH)
        prepared.append((k_heads, v_heads, allowed))

    def pair_scores(query_heads, k_heads):
        raw = jnp.einsum("ihd,jhd->hij", query_heads, k_heads, preferred_element_type=jnp.float32)
        return raw * scale + bias_col

    attended = jnp.zeros((row_count, head_count, DH), jnp.float32)
    for k_heads, v_heads, allowed in prepared:
        act, deriv = silu_parts(pair_scores(q_heads, k_heads))
        weights = jnp.where(allowed[None], act, 0.0).astype(jnp.bfloat16)
        attended = attended + jnp.einsum(
            "hij,jhd->ihd", weights, v_heads, preferred_element_type=jnp.float32
        )
    centered = attended - jnp.mean(attended, axis=-1, keepdims=True)
    inv_std = lax.rsqrt(jnp.mean(centered * centered, axis=-1, keepdims=True) + norm_eps)
    normed = centered * inv_std
    gate_heads = gates.reshape(row_count, head_count, DH).astype(jnp.float32)
    mixed = (normed * gate_heads).astype(jnp.bfloat16).reshape(row_count, feature_count)
    head_devices = lax.axis_size("head")
    head_index = lax.axis_index("head")
    partner = lax.ppermute(grad_out, "head", [(i, i ^ 1) for i in range(head_devices)])
    own_first = head_index % 2 == 0
    pair_block = jnp.where(
        own_first,
        jnp.concatenate([grad_out, partner], axis=1),
        jnp.concatenate([partner, grad_out], axis=1),
    )
    pair_count = head_devices // 2
    pair_index = head_index // 2
    gathered_blocks = [pair_block] + [
        lax.ppermute(
            pair_block, "head", [(i, (i + 2 * k) % head_devices) for i in range(head_devices)]
        )
        for k in range(1, pair_count)
    ]
    column_block = jnp.concatenate(gathered_blocks, axis=1)
    block_width = grad_out.shape[1]
    slot = jnp.arange(head_devices)
    source_block = 2 * ((pair_index - slot // 2) % pair_count) + slot % 2
    w_blocks = w_out.reshape(w_out.shape[0], head_devices, block_width)
    w_in_order = jnp.take(w_blocks, source_block, axis=1).reshape(w_out.shape)
    grad_mixed = lax.dot_general(
        column_block, w_in_order, (((1,), (1,)), ((), ())), preferred_element_type=jnp.float32
    )
    product = lax.dot_general(
        mixed, column_block, (((0,), (0,)), ((), ())), preferred_element_type=jnp.float32
    )
    weight_rows = jnp.take(
        product.reshape(product.shape[0], head_devices, block_width), source_block, axis=1
    ).reshape(product.shape)
    halving = halving_start(weight_rows, "seq")
    halving_levels = lax.axis_size("seq").bit_length() - 1
    grad_mixed = grad_mixed.reshape(row_count, head_count, DH)
    grad_gates = (grad_mixed * normed).reshape(row_count, feature_count)
    grad_normed = grad_mixed * gate_heads
    grad_attended = (
        grad_normed
        - jnp.mean(grad_normed, axis=-1, keepdims=True)
        - normed * jnp.mean(grad_normed * normed, axis=-1, keepdims=True)
    ) * inv_std
    grad_attended = grad_attended.astype(jnp.bfloat16)
    grad_queries = jnp.zeros((row_count, head_count, DH), jnp.float32)
    key_terms = []
    done_levels = 0
    for window_index in range(4):
        if window_index > 0 and done_levels < halving_levels:
            halving = halving_step(halving, "seq", done_levels)
            done_levels += 1
            halving, grad_attended = lax.optimization_barrier((halving, grad_attended))
        k_heads, v_heads, allowed = prepared[window_index]
        scores = pair_scores(q_heads, k_heads)
        key_act, key_deriv = silu_parts(scores)
        key_weights = jnp.where(allowed[None], key_act, 0.0).astype(jnp.bfloat16)
        values_term = jnp.einsum(
            "hij,ihd->jhd", key_weights, grad_attended, preferred_element_type=jnp.float32
        )
        grad_weights = jnp.einsum(
            "ihd,jhd->hij", grad_attended, v_heads, preferred_element_type=jnp.float32
        )
        grad_scores = jnp.where(allowed[None], grad_weights * key_deriv * scale, 0.0).astype(
            jnp.bfloat16
        )
        keys_term = jnp.einsum(
            "hij,ihd->jhd", grad_scores, q_heads, preferred_element_type=jnp.float32
        )
        grad_scores, term_pair = (
            grad_scores,
            jnp.stack(
                [
                    keys_term.reshape(row_count, feature_count),
                    values_term.reshape(row_count, feature_count),
                ]
            ),
        )
        key_terms.append(term_pair)
        grad_queries = grad_queries + jnp.einsum(
            "hij,jhd->ihd", grad_scores, k_heads, preferred_element_type=jnp.float32
        )
    summed = key_terms[0]
    for distance in back_steps:
        sent = shifted(key_terms[distance].astype(jnp.bfloat16), "seq", -distance)
        summed = summed + sent.astype(jnp.float32)
    while done_levels < halving_levels:
        halving = halving_step(halving, "seq", done_levels)
        done_levels += 1
    grad_w_out = halving.reshape(halving.shape[0], -1)
    return (
        grad_queries.reshape(row_count, feature_count),
        summed[0],
        summed[1],
        grad_gates,
        grad_w_out,
    )


def solution(mesh):
    return jax.shard_map(
        per_device,
        mesh=mesh,
        in_specs=(
            P("seq", "head"),
            P("seq", "head"),
            P("seq", "head"),
            P("seq", "head"),
            P("seq"),
            P("head"),
            P("seq", "head"),
            P("head", None),
        ),
        out_specs=(
            P("seq", "head"),
            P("seq", "head"),
            P("seq", "head"),
            P("seq", "head"),
            P("head", "seq"),
        ),
        check_vma=False,
    )
```

```python
import math

import jax
import jax.numpy as jnp
from jax import lax
from jax.sharding import PartitionSpec as P

DH = 128


back_steps = (1, 2, 3)
norm_eps = 1e-05


def shifted(block, axis, distance):
    devices = range(lax.axis_size(axis))
    route = [(i - distance, i) for i in devices if i - distance in devices]
    return lax.ppermute(block, axis, route)


def halving_start(block, axis):
    count = lax.axis_size(axis)
    rows, cols = block.shape
    levels = count.bit_length() - 1
    return block.reshape((rows,) + (2,) * levels + (cols // count,))


def radix_finish(current, axis, levels_done):
    count = lax.axis_size(axis)
    my_index = lax.axis_index(axis)
    low_count = 1 << levels_done
    high_count = count // low_count
    rows = current.shape[0]
    chunks = current.reshape(rows, high_count, -1)
    high = my_index // low_count
    rolled = jnp.take(chunks, (high + jnp.arange(high_count)) % high_count, axis=1)
    total = rolled[:, 0]
    for shift in range(1, high_count):
        route = [
            (i, ((i // low_count + shift) % high_count) * low_count + i % low_count)
            for i in range(count)
        ]
        total = total + lax.ppermute(rolled[:, shift], axis, route)
    return total


def halving_step(current, axis, level):
    count = lax.axis_size(axis)
    my_index = lax.axis_index(axis)
    bit = 1 << level
    axis_pos = current.ndim - 2
    mine = (my_index // bit) % 2
    low = lax.index_in_dim(current, 0, axis_pos, keepdims=False)
    high = lax.index_in_dim(current, 1, axis_pos, keepdims=False)
    keep = jnp.where(mine == 0, low, high)
    send = jnp.where(mine == 0, high, low)
    return keep + lax.ppermute(send, axis, [(i, i ^ bit) for i in range(count)])


def silu_parts(scores):
    sigma = jax.nn.sigmoid(scores)
    return (scores * sigma, sigma * (1.0 + scores * (1.0 - sigma)))


def per_device(queries, keys, values, gates, sessions, score_bias, grad_out, w_out):
    row_count = queries.shape[0]
    feature_count = queries.shape[1]
    head_count = feature_count // DH
    scale = 1.0 / math.sqrt(DH)
    my_index = lax.axis_index("seq")
    q_heads = queries.reshape(row_count, head_count, DH)
    bias_col = score_bias.reshape(head_count, 1, 1)
    offsets = jnp.arange(row_count, dtype=jnp.int32)
    session_rows = sessions.astype(jnp.bfloat16).reshape(-1, feature_count)
    packed = jnp.concatenate([keys, values, session_rows], axis=0)
    windows = [packed]
    for distance in back_steps:
        windows.append(shifted(packed, "seq", distance))
    prepared = []
    for distance in range(4):
        key_pack = windows[distance]
        if distance == 0:
            key_sessions = sessions
        else:
            key_sessions = key_pack[2 * row_count :].reshape(-1)[:row_count].astype(jnp.int32)
        allowed = (sessions[:, None] == key_sessions[None, :]) & (my_index >= distance)
        if distance == 0:
            allowed = allowed & (offsets[None, :] <= offsets[:, None])
        k_heads = key_pack[:row_count].reshape(row_count, head_count, DH)
        v_heads = key_pack[row_count : 2 * row_count].reshape(row_count, head_count, DH)
        prepared.append((k_heads, v_heads, allowed))

    def pair_scores(query_heads, k_heads):
        raw = jnp.einsum("ihd,jhd->hij", query_heads, k_heads, preferred_element_type=jnp.float32)
        return raw * scale + bias_col

    attended = jnp.zeros((row_count, head_count, DH), jnp.float32)
    for k_heads, v_heads, allowed in prepared:
        act, deriv = silu_parts(pair_scores(q_heads, k_heads))
        weights = jnp.where(allowed[None], act, 0.0).astype(jnp.bfloat16)
        attended = attended + jnp.einsum(
            "hij,jhd->ihd", weights, v_heads, preferred_element_type=jnp.float32
        )
    centered = attended - jnp.mean(attended, axis=-1, keepdims=True)
    inv_std = lax.rsqrt(jnp.mean(centered * centered, axis=-1, keepdims=True) + norm_eps)
    normed = centered * inv_std
    gate_heads = gates.reshape(row_count, head_count, DH).astype(jnp.float32)
    mixed = (normed * gate_heads).astype(jnp.bfloat16).reshape(row_count, feature_count)
    head_devices = lax.axis_size("head")
    head_index = lax.axis_index("head")
    partner = lax.ppermute(grad_out, "head", [(i, i ^ 1) for i in range(head_devices)])
    own_first = head_index % 2 == 0
    pair_block = jnp.where(
        own_first,
        jnp.concatenate([grad_out, partner], axis=1),
        jnp.concatenate([partner, grad_out], axis=1),
    )
    pair_count = head_devices // 2
    pair_index = head_index // 2
    gathered_blocks = [pair_block] + [
        lax.ppermute(
            pair_block, "head", [(i, (i + 2 * k) % head_devices) for i in range(head_devices)]
        )
        for k in range(1, pair_count)
    ]
    column_block = jnp.concatenate(gathered_blocks, axis=1)
    block_width = grad_out.shape[1]
    slot = jnp.arange(head_devices)
    source_block = 2 * ((pair_index - slot // 2) % pair_count) + slot % 2
    w_blocks = w_out.reshape(w_out.shape[0], head_devices, block_width)
    w_in_order = jnp.take(w_blocks, source_block, axis=1).reshape(w_out.shape)
    grad_mixed = lax.dot_general(
        column_block, w_in_order, (((1,), (1,)), ((), ())), preferred_element_type=jnp.float32
    )
    product = lax.dot_general(
        mixed, column_block, (((0,), (0,)), ((), ())), preferred_element_type=jnp.float32
    )
    weight_rows = jnp.take(
        product.reshape(product.shape[0], head_devices, block_width), source_block, axis=1
    ).reshape(product.shape)
    halving = halving_start(weight_rows, "seq")
    halving_levels = min(2, lax.axis_size("seq").bit_length() - 1)
    grad_mixed = grad_mixed.reshape(row_count, head_count, DH)
    grad_gates = (grad_mixed * normed).reshape(row_count, feature_count)
    grad_normed = grad_mixed * gate_heads
    grad_attended = (
        grad_normed
        - jnp.mean(grad_normed, axis=-1, keepdims=True)
        - normed * jnp.mean(grad_normed * normed, axis=-1, keepdims=True)
    ) * inv_std
    grad_attended = grad_attended.astype(jnp.bfloat16)
    grad_queries = jnp.zeros((row_count, head_count, DH), jnp.float32)
    key_terms = []
    done_levels = 0
    grad_w_out = None
    for window_index in range(4):
        if window_index > 0:
            if done_levels < halving_levels:
                halving = halving_step(halving, "seq", done_levels)
                done_levels += 1
                halving, grad_attended = lax.optimization_barrier((halving, grad_attended))
            elif grad_w_out is None:
                grad_w_out = radix_finish(halving, "seq", done_levels)
                grad_w_out, grad_attended = lax.optimization_barrier((grad_w_out, grad_attended))
        k_heads, v_heads, allowed = prepared[window_index]
        scores = pair_scores(q_heads, k_heads)
        key_act, key_deriv = silu_parts(scores)
        key_weights = jnp.where(allowed[None], key_act, 0.0).astype(jnp.bfloat16)
        values_term = jnp.einsum(
            "hij,ihd->jhd", key_weights, grad_attended, preferred_element_type=jnp.float32
        )
        grad_weights = jnp.einsum(
            "ihd,jhd->hij", grad_attended, v_heads, preferred_element_type=jnp.float32
        )
        grad_scores = jnp.where(allowed[None], grad_weights * key_deriv * scale, 0.0).astype(
            jnp.bfloat16
        )
        keys_term = jnp.einsum(
            "hij,ihd->jhd", grad_scores, q_heads, preferred_element_type=jnp.float32
        )
        grad_scores, term_pair = (
            grad_scores,
            jnp.stack(
                [
                    keys_term.reshape(row_count, feature_count),
                    values_term.reshape(row_count, feature_count),
                ]
            ),
        )
        key_terms.append(term_pair)
        grad_queries = grad_queries + jnp.einsum(
            "hij,jhd->ihd", grad_scores, k_heads, preferred_element_type=jnp.float32
        )
    summed = key_terms[0]
    for distance in back_steps:
        sent = shifted(key_terms[distance].astype(jnp.bfloat16), "seq", -distance)
        summed = summed + sent.astype(jnp.float32)
    while done_levels < halving_levels:
        halving = halving_step(halving, "seq", done_levels)
        done_levels += 1
    if grad_w_out is None:
        grad_w_out = radix_finish(halving, "seq", done_levels)
    return (
        grad_queries.reshape(row_count, feature_count),
        summed[0],
        summed[1],
        grad_gates,
        grad_w_out,
    )


def solution(mesh):
    return jax.shard_map(
        per_device,
        mesh=mesh,
        in_specs=(
            P("seq", "head"),
            P("seq", "head"),
            P("seq", "head"),
            P("seq", "head"),
            P("seq"),
            P("head"),
            P("seq", "head"),
            P("head", None),
        ),
        out_specs=(
            P("seq", "head"),
            P("seq", "head"),
            P("seq", "head"),
            P("seq", "head"),
            P("head", "seq"),
        ),
        check_vma=False,
    )
```

```python
import math

import jax
import jax.numpy as jnp
from jax import lax
from jax.sharding import PartitionSpec as P

DH = 128


back_steps = (1, 2, 3)
norm_eps = 1e-05


def shifted(block, axis, distance):
    devices = range(lax.axis_size(axis))
    route = [(i - distance, i) for i in devices if i - distance in devices]
    return lax.ppermute(block, axis, route)


def silu_parts(scores):
    sigma = jax.nn.sigmoid(scores)
    return (scores * sigma, sigma * (1.0 + scores * (1.0 - sigma)))


def per_device(queries, keys, values, gates, sessions, score_bias, grad_out, w_out):
    row_count = queries.shape[0]
    feature_count = queries.shape[1]
    head_count = feature_count // DH
    scale = 1.0 / math.sqrt(DH)
    my_index = lax.axis_index("seq")
    q_heads = queries.reshape(row_count, head_count, DH)
    bias_col = score_bias.reshape(head_count, 1, 1)
    offsets = jnp.arange(row_count, dtype=jnp.int32)
    session_rows = sessions.astype(jnp.bfloat16).reshape(-1, feature_count)
    packed = jnp.concatenate([keys, values, session_rows], axis=0)
    windows = [packed]
    for distance in back_steps:
        windows.append(shifted(packed, "seq", distance))
    prepared = []
    for distance in range(4):
        key_pack = windows[distance]
        if distance == 0:
            key_sessions = sessions
        else:
            key_sessions = key_pack[2 * row_count :].reshape(-1)[:row_count].astype(jnp.int32)
        allowed = (sessions[:, None] == key_sessions[None, :]) & (my_index >= distance)
        if distance == 0:
            allowed = allowed & (offsets[None, :] <= offsets[:, None])
        k_heads = key_pack[:row_count].reshape(row_count, head_count, DH)
        v_heads = key_pack[row_count : 2 * row_count].reshape(row_count, head_count, DH)
        prepared.append((k_heads, v_heads, allowed))

    def pair_scores(query_heads, k_heads):
        raw = jnp.einsum("ihd,jhd->hij", query_heads, k_heads, preferred_element_type=jnp.float32)
        return raw * scale + bias_col

    attended = jnp.zeros((row_count, head_count, DH), jnp.float32)
    for k_heads, v_heads, allowed in prepared:
        act, deriv = silu_parts(pair_scores(q_heads, k_heads))
        weights = jnp.where(allowed[None], act, 0.0).astype(jnp.bfloat16)
        attended = attended + jnp.einsum(
            "hij,jhd->ihd", weights, v_heads, preferred_element_type=jnp.float32
        )
    centered = attended - jnp.mean(attended, axis=-1, keepdims=True)
    inv_std = lax.rsqrt(jnp.mean(centered * centered, axis=-1, keepdims=True) + norm_eps)
    normed = centered * inv_std
    gate_heads = gates.reshape(row_count, head_count, DH).astype(jnp.float32)
    mixed = (normed * gate_heads).astype(jnp.bfloat16).reshape(row_count, feature_count)
    head_devices = lax.axis_size("head")
    head_index = lax.axis_index("head")
    partner = lax.ppermute(grad_out, "head", [(i, i ^ 1) for i in range(head_devices)])
    own_first = head_index % 2 == 0
    pair_block = jnp.where(
        own_first,
        jnp.concatenate([grad_out, partner], axis=1),
        jnp.concatenate([partner, grad_out], axis=1),
    )
    pair_count = head_devices // 2
    pair_index = head_index // 2
    gathered_blocks = [pair_block] + [
        lax.ppermute(
            pair_block, "head", [(i, (i + 2 * k) % head_devices) for i in range(head_devices)]
        )
        for k in range(1, pair_count)
    ]
    column_block = jnp.concatenate(gathered_blocks, axis=1)
    block_width = grad_out.shape[1]
    slot = jnp.arange(head_devices)
    source_block = 2 * ((pair_index - slot // 2) % pair_count) + slot % 2
    w_blocks = w_out.reshape(w_out.shape[0], head_devices, block_width)
    w_in_order = jnp.take(w_blocks, source_block, axis=1).reshape(w_out.shape)
    grad_mixed = lax.dot_general(
        column_block, w_in_order, (((1,), (1,)), ((), ())), preferred_element_type=jnp.float32
    )
    product = lax.dot_general(
        mixed, column_block, (((0,), (0,)), ((), ())), preferred_element_type=jnp.float32
    )
    weight_rows = jnp.take(
        product.reshape(product.shape[0], head_devices, block_width), source_block, axis=1
    ).reshape(product.shape)
    seq_n = lax.axis_size("seq")
    chunks = weight_rows.reshape(weight_rows.shape[0], seq_n, -1).transpose(1, 0, 2)
    exchanged = lax.all_to_all(chunks, "seq", 0, 0, tiled=True)
    grad_mixed = grad_mixed.reshape(row_count, head_count, DH)
    grad_gates = (grad_mixed * normed).reshape(row_count, feature_count)
    grad_normed = grad_mixed * gate_heads
    grad_attended = (
        grad_normed
        - jnp.mean(grad_normed, axis=-1, keepdims=True)
        - normed * jnp.mean(grad_normed * normed, axis=-1, keepdims=True)
    ) * inv_std
    grad_attended = grad_attended.astype(jnp.bfloat16)
    chunks, grad_attended = lax.optimization_barrier((chunks, grad_attended))
    grad_queries = jnp.zeros((row_count, head_count, DH), jnp.float32)
    key_terms = []
    for window_index in range(4):
        k_heads, v_heads, allowed = prepared[window_index]
        scores = pair_scores(q_heads, k_heads)
        key_act, key_deriv = silu_parts(scores)
        key_weights = jnp.where(allowed[None], key_act, 0.0).astype(jnp.bfloat16)
        values_term = jnp.einsum(
            "hij,ihd->jhd", key_weights, grad_attended, preferred_element_type=jnp.float32
        )
        grad_weights = jnp.einsum(
            "ihd,jhd->hij", grad_attended, v_heads, preferred_element_type=jnp.float32
        )
        grad_scores = jnp.where(allowed[None], grad_weights * key_deriv * scale, 0.0).astype(
            jnp.bfloat16
        )
        keys_term = jnp.einsum(
            "hij,ihd->jhd", grad_scores, q_heads, preferred_element_type=jnp.float32
        )
        grad_scores, term_pair = (
            grad_scores,
            jnp.stack(
                [
                    keys_term.reshape(row_count, feature_count),
                    values_term.reshape(row_count, feature_count),
                ]
            ),
        )
        key_terms.append(term_pair)
        grad_queries = grad_queries + jnp.einsum(
            "hij,jhd->ihd", grad_scores, k_heads, preferred_element_type=jnp.float32
        )
    summed = key_terms[0]
    for distance in back_steps:
        sent = shifted(key_terms[distance].astype(jnp.bfloat16), "seq", -distance)
        summed = summed + sent.astype(jnp.float32)
    grad_w_out = exchanged.sum(0)
    return (
        grad_queries.reshape(row_count, feature_count),
        summed[0],
        summed[1],
        grad_gates,
        grad_w_out,
    )


def solution(mesh):
    return jax.shard_map(
        per_device,
        mesh=mesh,
        in_specs=(
            P("seq", "head"),
            P("seq", "head"),
            P("seq", "head"),
            P("seq", "head"),
            P("seq"),
            P("head"),
            P("seq", "head"),
            P("head", None),
        ),
        out_specs=(
            P("seq", "head"),
            P("seq", "head"),
            P("seq", "head"),
            P("seq", "head"),
            P("head", "seq"),
        ),
        check_vma=False,
    )
```

```python
import math

import jax
import jax.numpy as jnp
from jax import lax
from jax.sharding import PartitionSpec as P

DH = 128


back_steps = (1, 2, 3)
norm_eps = 1e-05


def shifted(block, axis, distance):
    devices = range(lax.axis_size(axis))
    route = [(i - distance, i) for i in devices if i - distance in devices]
    return lax.ppermute(block, axis, route)


def halving_start(block, axis):
    count = lax.axis_size(axis)
    rows, cols = block.shape
    levels = count.bit_length() - 1
    return block.reshape((rows,) + (2,) * levels + (cols // count,))


def halving_step(current, axis, level):
    count = lax.axis_size(axis)
    my_index = lax.axis_index(axis)
    bit = 1 << level
    axis_pos = current.ndim - 2
    mine = (my_index // bit) % 2
    low = lax.index_in_dim(current, 0, axis_pos, keepdims=False)
    high = lax.index_in_dim(current, 1, axis_pos, keepdims=False)
    keep = jnp.where(mine == 0, low, high)
    send = jnp.where(mine == 0, high, low)
    return keep + lax.ppermute(send, axis, [(i, i ^ bit) for i in range(count)])


def silu_parts(scores):
    sigma = jax.nn.sigmoid(scores)
    return (scores * sigma, sigma * (1.0 + scores * (1.0 - sigma)))


def per_device(queries, keys, values, gates, sessions, score_bias, grad_out, w_out):
    row_count = queries.shape[0]
    feature_count = queries.shape[1]
    head_count = feature_count // DH
    scale = 1.0 / math.sqrt(DH)
    my_index = lax.axis_index("seq")
    q_heads = queries.reshape(row_count, head_count, DH)
    bias_col = score_bias.reshape(head_count, 1, 1)
    offsets = jnp.arange(row_count, dtype=jnp.int32)
    session_rows = sessions.astype(jnp.bfloat16).reshape(-1, feature_count)
    packed = jnp.concatenate([keys, values, session_rows], axis=0)
    windows = [packed]
    for distance in back_steps:
        windows.append(shifted(packed, "seq", distance))
    prepared = []
    for distance in range(4):
        key_pack = windows[distance]
        if distance == 0:
            key_sessions = sessions
        else:
            key_sessions = key_pack[2 * row_count :].reshape(-1)[:row_count].astype(jnp.int32)
        allowed = (sessions[:, None] == key_sessions[None, :]) & (my_index >= distance)
        if distance == 0:
            allowed = allowed & (offsets[None, :] <= offsets[:, None])
        k_heads = key_pack[:row_count].reshape(row_count, head_count, DH)
        v_heads = key_pack[row_count : 2 * row_count].reshape(row_count, head_count, DH)
        prepared.append((k_heads, v_heads, allowed))

    def pair_scores(query_heads, k_heads):
        raw = jnp.einsum("ihd,jhd->hij", query_heads, k_heads, preferred_element_type=jnp.float32)
        return raw * scale + bias_col

    attended = jnp.zeros((row_count, head_count, DH), jnp.float32)
    for k_heads, v_heads, allowed in prepared:
        act, deriv = silu_parts(pair_scores(q_heads, k_heads))
        weights = jnp.where(allowed[None], act, 0.0).astype(jnp.bfloat16)
        attended = attended + jnp.einsum(
            "hij,jhd->ihd", weights, v_heads, preferred_element_type=jnp.float32
        )
    centered = attended - jnp.mean(attended, axis=-1, keepdims=True)
    inv_std = lax.rsqrt(jnp.mean(centered * centered, axis=-1, keepdims=True) + norm_eps)
    normed = centered * inv_std
    gate_heads = gates.reshape(row_count, head_count, DH).astype(jnp.float32)
    mixed = (normed * gate_heads).astype(jnp.bfloat16).reshape(row_count, feature_count)
    head_devices = lax.axis_size("head")
    head_index = lax.axis_index("head")
    partner = lax.ppermute(grad_out, "head", [(i, i ^ 1) for i in range(head_devices)])
    own_first = head_index % 2 == 0
    pair_block = jnp.where(
        own_first,
        jnp.concatenate([grad_out, partner], axis=1),
        jnp.concatenate([partner, grad_out], axis=1),
    )
    pair_count = head_devices // 2
    pair_index = head_index // 2
    gathered_blocks = [pair_block] + [
        lax.ppermute(
            pair_block, "head", [(i, (i + 2 * k) % head_devices) for i in range(head_devices)]
        )
        for k in range(1, pair_count)
    ]
    column_block = jnp.concatenate(gathered_blocks, axis=1)
    block_width = grad_out.shape[1]
    slot = jnp.arange(head_devices)
    source_block = 2 * ((pair_index - slot // 2) % pair_count) + slot % 2
    w_blocks = w_out.reshape(w_out.shape[0], head_devices, block_width)
    w_in_order = jnp.take(w_blocks, source_block, axis=1).reshape(w_out.shape)
    grad_mixed = lax.dot_general(
        column_block, w_in_order, (((1,), (1,)), ((), ())), preferred_element_type=jnp.float32
    )
    product = lax.dot_general(
        mixed, column_block, (((0,), (0,)), ((), ())), preferred_element_type=jnp.float32
    )
    weight_rows = jnp.take(
        product.reshape(product.shape[0], head_devices, block_width), source_block, axis=1
    ).reshape(product.shape)
    halving = halving_start(weight_rows, "seq")
    halving_levels = lax.axis_size("seq").bit_length() - 1
    grad_mixed = grad_mixed.reshape(row_count, head_count, DH)
    grad_gates = (grad_mixed * normed).reshape(row_count, feature_count)
    grad_normed = grad_mixed * gate_heads
    grad_attended = (
        grad_normed
        - jnp.mean(grad_normed, axis=-1, keepdims=True)
        - normed * jnp.mean(grad_normed * normed, axis=-1, keepdims=True)
    ) * inv_std
    grad_attended = grad_attended.astype(jnp.bfloat16)
    grad_queries = jnp.zeros((row_count, head_count, DH), jnp.float32)
    key_terms = [None] * 4
    done_levels = 0
    for step_index, window_index in enumerate((3, 2, 1, 0)):
        if step_index > 0 and done_levels < halving_levels:
            halving = halving_step(halving, "seq", done_levels)
            done_levels += 1
            halving, grad_attended = lax.optimization_barrier((halving, grad_attended))
        k_heads, v_heads, allowed = prepared[window_index]
        scores = pair_scores(q_heads, k_heads)
        key_act, key_deriv = silu_parts(scores)
        key_weights = jnp.where(allowed[None], key_act, 0.0).astype(jnp.bfloat16)
        values_term = jnp.einsum(
            "hij,ihd->jhd", key_weights, grad_attended, preferred_element_type=jnp.float32
        )
        grad_weights = jnp.einsum(
            "ihd,jhd->hij", grad_attended, v_heads, preferred_element_type=jnp.float32
        )
        grad_scores = jnp.where(allowed[None], grad_weights * key_deriv * scale, 0.0).astype(
            jnp.bfloat16
        )
        keys_term = jnp.einsum(
            "hij,ihd->jhd", grad_scores, q_heads, preferred_element_type=jnp.float32
        )
        grad_scores, term_pair = (
            grad_scores,
            jnp.stack(
                [
                    keys_term.reshape(row_count, feature_count),
                    values_term.reshape(row_count, feature_count),
                ]
            ),
        )
        key_terms[window_index] = term_pair
        if window_index > 0:
            key_terms[window_index] = shifted(
                term_pair.astype(jnp.bfloat16), "seq", -window_index
            ).astype(jnp.float32)
        grad_queries = grad_queries + jnp.einsum(
            "hij,jhd->ihd", grad_scores, k_heads, preferred_element_type=jnp.float32
        )
    summed = key_terms[0]
    for distance in back_steps:
        summed = summed + key_terms[distance]
    while done_levels < halving_levels:
        halving = halving_step(halving, "seq", done_levels)
        done_levels += 1
    grad_w_out = halving.reshape(halving.shape[0], -1)
    return (
        grad_queries.reshape(row_count, feature_count),
        summed[0],
        summed[1],
        grad_gates,
        grad_w_out,
    )


def solution(mesh):
    return jax.shard_map(
        per_device,
        mesh=mesh,
        in_specs=(
            P("seq", "head"),
            P("seq", "head"),
            P("seq", "head"),
            P("seq", "head"),
            P("seq"),
            P("head"),
            P("seq", "head"),
            P("head", None),
        ),
        out_specs=(
            P("seq", "head"),
            P("seq", "head"),
            P("seq", "head"),
            P("seq", "head"),
            P("head", "seq"),
        ),
        check_vma=False,
    )
```

```python
import math

import jax
import jax.numpy as jnp
from jax import lax
from jax.sharding import PartitionSpec as P

DH = 128


back_steps = (1, 2, 3)
norm_eps = 1e-05


def shifted(block, axis, distance):
    devices = range(lax.axis_size(axis))
    route = [(i - distance, i) for i in devices if i - distance in devices]
    return lax.ppermute(block, axis, route)


def halving_start(block, axis):
    count = lax.axis_size(axis)
    rows, cols = block.shape
    levels = count.bit_length() - 1
    return block.reshape((rows,) + (2,) * levels + (cols // count,))


def halving_step(current, axis, level):
    count = lax.axis_size(axis)
    my_index = lax.axis_index(axis)
    bit = 1 << level
    axis_pos = current.ndim - 2
    mine = (my_index // bit) % 2
    low = lax.index_in_dim(current, 0, axis_pos, keepdims=False)
    high = lax.index_in_dim(current, 1, axis_pos, keepdims=False)
    keep = jnp.where(mine == 0, low, high)
    send = jnp.where(mine == 0, high, low)
    return keep + lax.ppermute(send, axis, [(i, i ^ bit) for i in range(count)])


def silu_parts(scores):
    sigma = jax.nn.sigmoid(scores)
    return (scores * sigma, sigma * (1.0 + scores * (1.0 - sigma)))


def per_device(queries, keys, values, gates, sessions, score_bias, grad_out, w_out):
    row_count = queries.shape[0]
    feature_count = queries.shape[1]
    head_count = feature_count // DH
    scale = 1.0 / math.sqrt(DH)
    my_index = lax.axis_index("seq")
    q_heads = queries.reshape(row_count, head_count, DH)
    bias_col = score_bias.reshape(head_count, 1, 1)
    offsets = jnp.arange(row_count, dtype=jnp.int32)
    session_rows = sessions.astype(jnp.bfloat16).reshape(-1, feature_count)
    packed = jnp.concatenate([keys, values, session_rows], axis=0)
    windows = [packed]
    for distance in back_steps:
        windows.append(shifted(packed, "seq", distance))
    prepared = []
    for distance in range(4):
        key_pack = windows[distance]
        if distance == 0:
            key_sessions = sessions
        else:
            key_sessions = key_pack[2 * row_count :].reshape(-1)[:row_count].astype(jnp.int32)
        allowed = (sessions[:, None] == key_sessions[None, :]) & (my_index >= distance)
        if distance == 0:
            allowed = allowed & (offsets[None, :] <= offsets[:, None])
        k_heads = key_pack[:row_count].reshape(row_count, head_count, DH)
        v_heads = key_pack[row_count : 2 * row_count].reshape(row_count, head_count, DH)
        prepared.append((k_heads, v_heads, allowed))

    def pair_scores(query_heads, k_heads):
        raw = jnp.einsum("ihd,jhd->hij", query_heads, k_heads, preferred_element_type=jnp.float32)
        return raw * scale + bias_col

    attended = jnp.zeros((row_count, head_count, DH), jnp.float32)
    for k_heads, v_heads, allowed in prepared:
        act, deriv = silu_parts(pair_scores(q_heads, k_heads))
        weights = jnp.where(allowed[None], act, 0.0).astype(jnp.bfloat16)
        attended = attended + jnp.einsum(
            "hij,jhd->ihd", weights, v_heads, preferred_element_type=jnp.float32
        )
    centered = attended - jnp.mean(attended, axis=-1, keepdims=True)
    inv_std = lax.rsqrt(jnp.mean(centered * centered, axis=-1, keepdims=True) + norm_eps)
    normed = centered * inv_std
    gate_heads = gates.reshape(row_count, head_count, DH).astype(jnp.float32)
    mixed = (normed * gate_heads).astype(jnp.bfloat16).reshape(row_count, feature_count)
    head_devices = lax.axis_size("head")
    head_index = lax.axis_index("head")
    partner = lax.ppermute(grad_out, "head", [(i, i ^ 1) for i in range(head_devices)])
    own_first = head_index % 2 == 0
    pair_block = jnp.where(
        own_first,
        jnp.concatenate([grad_out, partner], axis=1),
        jnp.concatenate([partner, grad_out], axis=1),
    )
    pair_count = head_devices // 2
    pair_index = head_index // 2
    gathered_blocks = [pair_block] + [
        lax.ppermute(
            pair_block, "head", [(i, (i + 2 * k) % head_devices) for i in range(head_devices)]
        )
        for k in range(1, pair_count)
    ]
    block_width = grad_out.shape[1]
    slot = jnp.arange(head_devices)
    source_block = 2 * ((pair_index - slot // 2) % pair_count) + slot % 2
    w_blocks = w_out.reshape(w_out.shape[0], head_devices, block_width)
    w_in_order = jnp.take(w_blocks, source_block, axis=1).reshape(
        w_out.shape[0], len(gathered_blocks), -1
    )
    grad_mixed = sum(
        lax.dot_general(
            gathered, w_in_order[:, k], (((1,), (1,)), ((), ())), preferred_element_type=jnp.float32
        )
        for k, gathered in enumerate(gathered_blocks)
    )
    product = jnp.concatenate(
        [
            lax.dot_general(
                mixed, gathered, (((0,), (0,)), ((), ())), preferred_element_type=jnp.float32
            )
            for gathered in gathered_blocks
        ],
        axis=1,
    )
    weight_rows = jnp.take(
        product.reshape(product.shape[0], head_devices, block_width), source_block, axis=1
    ).reshape(product.shape)
    halving = halving_start(weight_rows, "seq")
    halving_levels = lax.axis_size("seq").bit_length() - 1
    grad_mixed = grad_mixed.reshape(row_count, head_count, DH)
    grad_gates = (grad_mixed * normed).reshape(row_count, feature_count)
    grad_normed = grad_mixed * gate_heads
    grad_attended = (
        grad_normed
        - jnp.mean(grad_normed, axis=-1, keepdims=True)
        - normed * jnp.mean(grad_normed * normed, axis=-1, keepdims=True)
    ) * inv_std
    grad_attended = grad_attended.astype(jnp.bfloat16)
    grad_queries = jnp.zeros((row_count, head_count, DH), jnp.float32)
    key_terms = []
    done_levels = 0
    for window_index in range(4):
        if window_index > 0 and done_levels < halving_levels:
            halving = halving_step(halving, "seq", done_levels)
            done_levels += 1
            halving, grad_attended = lax.optimization_barrier((halving, grad_attended))
        k_heads, v_heads, allowed = prepared[window_index]
        scores = pair_scores(q_heads, k_heads)
        key_act, key_deriv = silu_parts(scores)
        key_weights = jnp.where(allowed[None], key_act, 0.0).astype(jnp.bfloat16)
        values_term = jnp.einsum(
            "hij,ihd->jhd", key_weights, grad_attended, preferred_element_type=jnp.float32
        )
        grad_weights = jnp.einsum(
            "ihd,jhd->hij", grad_attended, v_heads, preferred_element_type=jnp.float32
        )
        grad_scores = jnp.where(allowed[None], grad_weights * key_deriv * scale, 0.0).astype(
            jnp.bfloat16
        )
        keys_term = jnp.einsum(
            "hij,ihd->jhd", grad_scores, q_heads, preferred_element_type=jnp.float32
        )
        grad_scores, term_pair = (
            grad_scores,
            jnp.stack(
                [
                    keys_term.reshape(row_count, feature_count),
                    values_term.reshape(row_count, feature_count),
                ]
            ),
        )
        key_terms.append(term_pair)
        grad_queries = grad_queries + jnp.einsum(
            "hij,jhd->ihd", grad_scores, k_heads, preferred_element_type=jnp.float32
        )
    summed = key_terms[0]
    for distance in back_steps:
        sent = shifted(key_terms[distance].astype(jnp.bfloat16), "seq", -distance)
        summed = summed + sent.astype(jnp.float32)
    while done_levels < halving_levels:
        halving = halving_step(halving, "seq", done_levels)
        done_levels += 1
    grad_w_out = halving.reshape(halving.shape[0], -1)
    return (
        grad_queries.reshape(row_count, feature_count),
        summed[0],
        summed[1],
        grad_gates,
        grad_w_out,
    )


def solution(mesh):
    return jax.shard_map(
        per_device,
        mesh=mesh,
        in_specs=(
            P("seq", "head"),
            P("seq", "head"),
            P("seq", "head"),
            P("seq", "head"),
            P("seq"),
            P("head"),
            P("seq", "head"),
            P("head", None),
        ),
        out_specs=(
            P("seq", "head"),
            P("seq", "head"),
            P("seq", "head"),
            P("seq", "head"),
            P("head", "seq"),
        ),
        check_vma=False,
    )
```

```python
import math

import jax
import jax.numpy as jnp
from jax import lax
from jax.sharding import PartitionSpec as P


DH = 128


back_steps = (1, 2, 3)
norm_eps = 1e-05


def shifted(block, axis, distance):
    devices = range(lax.axis_size(axis))
    route = [(i - distance, i) for i in devices if i - distance in devices]
    return lax.ppermute(block, axis, route)


def halving_start(block, axis):
    count = lax.axis_size(axis)
    rows, cols = block.shape
    levels = count.bit_length() - 1
    return block.reshape((rows,) + (2,) * levels + (cols // count,))


def halving_step(current, axis, level):
    count = lax.axis_size(axis)
    my_index = lax.axis_index(axis)
    levels = count.bit_length() - 1
    bit = 1 << (levels - 1 - level)
    axis_pos = 1
    mine = (my_index // bit) % 2
    low = lax.index_in_dim(current, 0, axis_pos, keepdims=False)
    high = lax.index_in_dim(current, 1, axis_pos, keepdims=False)
    keep = jnp.where(mine == 0, low, high)
    send = jnp.where(mine == 0, high, low)
    return keep + lax.ppermute(send, axis, [(i, i ^ bit) for i in range(count)])


def silu_parts(scores):
    sigma = jax.nn.sigmoid(scores)
    return (scores * sigma, sigma * (1.0 + scores * (1.0 - sigma)))


def per_device(queries, keys, values, gates, sessions, score_bias, grad_out, w_out):
    row_count = queries.shape[0]
    feature_count = queries.shape[1]
    head_count = feature_count // DH
    scale = 1.0 / math.sqrt(DH)
    my_index = lax.axis_index("seq")
    q_heads = queries.reshape(row_count, head_count, DH)
    bias_col = score_bias.reshape(head_count, 1, 1)
    offsets = jnp.arange(row_count, dtype=jnp.int32)
    session_rows = sessions.astype(jnp.bfloat16).reshape(-1, feature_count)
    packed = jnp.concatenate([keys, values, session_rows], axis=0)
    windows = [packed]
    for distance in back_steps:
        windows.append(shifted(packed, "seq", distance))
    prepared = []
    for distance in range(4):
        key_pack = windows[distance]
        if distance == 0:
            key_sessions = sessions
        else:
            key_sessions = key_pack[2 * row_count :].reshape(-1)[:row_count].astype(jnp.int32)
        allowed = (sessions[:, None] == key_sessions[None, :]) & (my_index >= distance)
        if distance == 0:
            allowed = allowed & (offsets[None, :] <= offsets[:, None])
        k_heads = key_pack[:row_count].reshape(row_count, head_count, DH)
        v_heads = key_pack[row_count : 2 * row_count].reshape(row_count, head_count, DH)
        prepared.append((k_heads, v_heads, allowed))

    def pair_scores(query_heads, k_heads):
        raw = jnp.einsum("ihd,jhd->hij", query_heads, k_heads, preferred_element_type=jnp.float32)
        return raw * scale + bias_col

    attended = jnp.zeros((row_count, head_count, DH), jnp.float32)
    for k_heads, v_heads, allowed in prepared:
        act, _ = silu_parts(pair_scores(q_heads, k_heads))
        weights = jnp.where(allowed[None], act, 0.0).astype(jnp.bfloat16)
        attended = attended + jnp.einsum(
            "hij,jhd->ihd", weights, v_heads, preferred_element_type=jnp.float32
        )
    centered = attended - jnp.mean(attended, axis=-1, keepdims=True)
    inv_std = lax.rsqrt(jnp.mean(centered * centered, axis=-1, keepdims=True) + norm_eps)
    normed = centered * inv_std
    gate_heads = gates.reshape(row_count, head_count, DH).astype(jnp.float32)
    mixed = (normed * gate_heads).astype(jnp.bfloat16).reshape(row_count, feature_count)
    head_devices = lax.axis_size("head")
    head_index = lax.axis_index("head")
    partner = lax.ppermute(grad_out, "head", [(i, i ^ 1) for i in range(head_devices)])
    own_first = head_index % 2 == 0
    pair_block = jnp.where(
        own_first,
        jnp.concatenate([grad_out, partner], axis=1),
        jnp.concatenate([partner, grad_out], axis=1),
    )
    pair_count = head_devices // 2
    pair_index = head_index // 2
    gathered_blocks = [pair_block] + [
        lax.ppermute(
            pair_block, "head", [(i, (i + 2 * k) % head_devices) for i in range(head_devices)]
        )
        for k in range(1, pair_count)
    ]
    block_width = grad_out.shape[1]
    slot = jnp.arange(head_devices)
    source_block = 2 * ((pair_index - slot // 2) % pair_count) + slot % 2
    w_blocks = w_out.reshape(w_out.shape[0], head_devices, block_width)
    w_in_order = jnp.take(w_blocks, source_block, axis=1).reshape(
        w_out.shape[0], len(gathered_blocks), -1
    )
    grad_mixed = sum(
        lax.dot_general(
            gathered, w_in_order[:, k], (((1,), (1,)), ((), ())), preferred_element_type=jnp.float32
        )
        for k, gathered in enumerate(gathered_blocks)
    )
    product = jnp.concatenate(
        [
            lax.dot_general(
                mixed, gathered, (((0,), (0,)), ((), ())), preferred_element_type=jnp.float32
            )
            for gathered in gathered_blocks
        ],
        axis=1,
    )
    weight_rows = jnp.take(
        product.reshape(product.shape[0], head_devices, block_width), source_block, axis=1
    ).reshape(product.shape)
    halving = halving_start(weight_rows, "seq")
    halving_levels = lax.axis_size("seq").bit_length() - 1
    grad_mixed = grad_mixed.reshape(row_count, head_count, DH)
    grad_gates = (grad_mixed * normed).reshape(row_count, feature_count)
    grad_normed = grad_mixed * gate_heads
    grad_attended = (
        grad_normed
        - jnp.mean(grad_normed, axis=-1, keepdims=True)
        - normed * jnp.mean(grad_normed * normed, axis=-1, keepdims=True)
    ) * inv_std
    grad_attended = grad_attended.astype(jnp.bfloat16)
    grad_queries = jnp.zeros((row_count, head_count, DH), jnp.float32)
    key_terms = []
    done_levels = 0
    for window_index in range(4):
        if window_index > 0 and done_levels < halving_levels:
            halving = halving_step(halving, "seq", done_levels)
            done_levels += 1
            halving, grad_attended = lax.optimization_barrier((halving, grad_attended))
        k_heads, v_heads, allowed = prepared[window_index]
        scores = pair_scores(q_heads, k_heads)
        key_act, key_deriv = silu_parts(scores)
        key_weights = jnp.where(allowed[None], key_act, 0.0).astype(jnp.bfloat16)
        values_term = jnp.einsum(
            "hij,ihd->jhd", key_weights, grad_attended, preferred_element_type=jnp.float32
        )
        grad_weights = jnp.einsum(
            "ihd,jhd->hij", grad_attended, v_heads, preferred_element_type=jnp.float32
        )
        grad_scores = jnp.where(allowed[None], grad_weights * key_deriv * scale, 0.0).astype(
            jnp.bfloat16
        )
        keys_term = jnp.einsum(
            "hij,ihd->jhd", grad_scores, q_heads, preferred_element_type=jnp.float32
        )
        grad_scores, term_pair = (
            grad_scores,
            jnp.stack(
                [
                    keys_term.reshape(row_count, feature_count),
                    values_term.reshape(row_count, feature_count),
                ]
            ),
        )
        key_terms.append(term_pair)
        grad_queries = grad_queries + jnp.einsum(
            "hij,jhd->ihd", grad_scores, k_heads, preferred_element_type=jnp.float32
        )
    summed = key_terms[0]
    for distance in back_steps:
        sent = shifted(key_terms[distance].astype(jnp.bfloat16), "seq", -distance)
        summed = summed + sent.astype(jnp.float32)
    while done_levels < halving_levels:
        halving = halving_step(halving, "seq", done_levels)
        done_levels += 1
    grad_w_out = halving.reshape(halving.shape[0], -1)
    return (
        grad_queries.reshape(row_count, feature_count),
        summed[0],
        summed[1],
        grad_gates,
        grad_w_out,
    )


def solution(mesh):
    return jax.shard_map(
        per_device,
        mesh=mesh,
        in_specs=(
            P("seq", "head"),
            P("seq", "head"),
            P("seq", "head"),
            P("seq", "head"),
            P("seq"),
            P("head"),
            P("seq", "head"),
            P("head", None),
        ),
        out_specs=(
            P("seq", "head"),
            P("seq", "head"),
            P("seq", "head"),
            P("seq", "head"),
            P("head", "seq"),
        ),
        check_vma=False,
    )
```

```python
import math

import jax
import jax.numpy as jnp
from jax import lax
from jax.sharding import PartitionSpec as P


DH = 128


back_steps = (1, 2, 3)
norm_eps = 1e-05


def shifted(block, axis, distance):
    devices = range(lax.axis_size(axis))
    route = [(i - distance, i) for i in devices if i - distance in devices]
    return lax.ppermute(block, axis, route)


def halving_start(block, axis):
    count = lax.axis_size(axis)
    rows, cols = block.shape
    levels = count.bit_length() - 1
    return block.reshape((rows,) + (2,) * levels + (cols // count,))


def halving_step(current, axis, level):
    count = lax.axis_size(axis)
    my_index = lax.axis_index(axis)
    levels = count.bit_length() - 1
    order = [0] + list(range(levels - 1, 0, -1))
    bit = 1 << order[level]
    remaining = sorted(order[level:], reverse=True)
    axis_pos = 1 + remaining.index(order[level])
    mine = (my_index // bit) % 2
    low = lax.index_in_dim(current, 0, axis_pos, keepdims=False)
    high = lax.index_in_dim(current, 1, axis_pos, keepdims=False)
    keep = jnp.where(mine == 0, low, high)
    send = jnp.where(mine == 0, high, low)
    return keep + lax.ppermute(send, axis, [(i, i ^ bit) for i in range(count)])


def silu_parts(scores):
    sigma = jax.nn.sigmoid(scores)
    return (scores * sigma, sigma * (1.0 + scores * (1.0 - sigma)))


def per_device(queries, keys, values, gates, sessions, score_bias, grad_out, w_out):
    row_count = queries.shape[0]
    feature_count = queries.shape[1]
    head_count = feature_count // DH
    scale = 1.0 / math.sqrt(DH)
    my_index = lax.axis_index("seq")
    q_heads = queries.reshape(row_count, head_count, DH)
    bias_col = score_bias.reshape(head_count, 1, 1)
    offsets = jnp.arange(row_count, dtype=jnp.int32)
    session_rows = sessions.astype(jnp.bfloat16).reshape(-1, feature_count)
    packed = jnp.concatenate([keys, values, session_rows], axis=0)
    windows = [packed]
    for distance in back_steps:
        windows.append(shifted(packed, "seq", distance))
    prepared = []
    for distance in range(4):
        key_pack = windows[distance]
        if distance == 0:
            key_sessions = sessions
        else:
            key_sessions = key_pack[2 * row_count :].reshape(-1)[:row_count].astype(jnp.int32)
        allowed = (sessions[:, None] == key_sessions[None, :]) & (my_index >= distance)
        if distance == 0:
            allowed = allowed & (offsets[None, :] <= offsets[:, None])
        k_heads = key_pack[:row_count].reshape(row_count, head_count, DH)
        v_heads = key_pack[row_count : 2 * row_count].reshape(row_count, head_count, DH)
        prepared.append((k_heads, v_heads, allowed))

    def pair_scores(query_heads, k_heads):
        raw = jnp.einsum("ihd,jhd->hij", query_heads, k_heads, preferred_element_type=jnp.float32)
        return raw * scale + bias_col

    attended = jnp.zeros((row_count, head_count, DH), jnp.float32)
    for k_heads, v_heads, allowed in prepared:
        act, _ = silu_parts(pair_scores(q_heads, k_heads))
        weights = jnp.where(allowed[None], act, 0.0).astype(jnp.bfloat16)
        attended = attended + jnp.einsum(
            "hij,jhd->ihd", weights, v_heads, preferred_element_type=jnp.float32
        )
    centered = attended - jnp.mean(attended, axis=-1, keepdims=True)
    inv_std = lax.rsqrt(jnp.mean(centered * centered, axis=-1, keepdims=True) + norm_eps)
    normed = centered * inv_std
    gate_heads = gates.reshape(row_count, head_count, DH).astype(jnp.float32)
    mixed = (normed * gate_heads).astype(jnp.bfloat16).reshape(row_count, feature_count)
    head_devices = lax.axis_size("head")
    head_index = lax.axis_index("head")
    partner = lax.ppermute(grad_out, "head", [(i, i ^ 1) for i in range(head_devices)])
    own_first = head_index % 2 == 0
    pair_block = jnp.where(
        own_first,
        jnp.concatenate([grad_out, partner], axis=1),
        jnp.concatenate([partner, grad_out], axis=1),
    )
    pair_count = head_devices // 2
    pair_index = head_index // 2
    gathered_blocks = [pair_block] + [
        lax.ppermute(
            pair_block, "head", [(i, (i + 2 * k) % head_devices) for i in range(head_devices)]
        )
        for k in range(1, pair_count)
    ]
    block_width = grad_out.shape[1]
    slot = jnp.arange(head_devices)
    source_block = 2 * ((pair_index - slot // 2) % pair_count) + slot % 2
    w_blocks = w_out.reshape(w_out.shape[0], head_devices, block_width)
    w_in_order = jnp.take(w_blocks, source_block, axis=1).reshape(
        w_out.shape[0], len(gathered_blocks), -1
    )
    grad_mixed = sum(
        lax.dot_general(
            gathered, w_in_order[:, k], (((1,), (1,)), ((), ())), preferred_element_type=jnp.float32
        )
        for k, gathered in enumerate(gathered_blocks)
    )
    product = jnp.concatenate(
        [
            lax.dot_general(
                mixed, gathered, (((0,), (0,)), ((), ())), preferred_element_type=jnp.float32
            )
            for gathered in gathered_blocks
        ],
        axis=1,
    )
    weight_rows = jnp.take(
        product.reshape(product.shape[0], head_devices, block_width), source_block, axis=1
    ).reshape(product.shape)
    halving = halving_start(weight_rows, "seq")
    halving_levels = lax.axis_size("seq").bit_length() - 1
    grad_mixed = grad_mixed.reshape(row_count, head_count, DH)
    grad_gates = (grad_mixed * normed).reshape(row_count, feature_count)
    grad_normed = grad_mixed * gate_heads
    grad_attended = (
        grad_normed
        - jnp.mean(grad_normed, axis=-1, keepdims=True)
        - normed * jnp.mean(grad_normed * normed, axis=-1, keepdims=True)
    ) * inv_std
    grad_attended = grad_attended.astype(jnp.bfloat16)
    grad_queries = jnp.zeros((row_count, head_count, DH), jnp.float32)
    key_terms = []
    done_levels = 0
    for window_index in range(4):
        if window_index > 0 and done_levels < halving_levels:
            if done_levels == 1:
                halving, grad_queries = lax.optimization_barrier((halving, grad_queries))
            halving = halving_step(halving, "seq", done_levels)
            done_levels += 1
            halving, grad_attended = lax.optimization_barrier((halving, grad_attended))
        k_heads, v_heads, allowed = prepared[window_index]
        scores = pair_scores(q_heads, k_heads)
        key_act, key_deriv = silu_parts(scores)
        key_weights = jnp.where(allowed[None], key_act, 0.0).astype(jnp.bfloat16)
        values_term = jnp.einsum(
            "hij,ihd->jhd", key_weights, grad_attended, preferred_element_type=jnp.float32
        )
        grad_weights = jnp.einsum(
            "ihd,jhd->hij", grad_attended, v_heads, preferred_element_type=jnp.float32
        )
        grad_scores = jnp.where(allowed[None], grad_weights * key_deriv * scale, 0.0).astype(
            jnp.bfloat16
        )
        keys_term = jnp.einsum(
            "hij,ihd->jhd", grad_scores, q_heads, preferred_element_type=jnp.float32
        )
        grad_scores, term_pair = (
            grad_scores,
            jnp.stack(
                [
                    keys_term.reshape(row_count, feature_count),
                    values_term.reshape(row_count, feature_count),
                ]
            ),
        )
        key_terms.append(term_pair)
        grad_queries = grad_queries + jnp.einsum(
            "hij,jhd->ihd", grad_scores, k_heads, preferred_element_type=jnp.float32
        )
    summed = key_terms[0]
    for distance in back_steps:
        sent = shifted(key_terms[distance].astype(jnp.bfloat16), "seq", -distance)
        summed = summed + sent.astype(jnp.float32)
    while done_levels < halving_levels:
        halving = halving_step(halving, "seq", done_levels)
        done_levels += 1
    grad_w_out = halving.reshape(halving.shape[0], -1)
    return (
        grad_queries.reshape(row_count, feature_count),
        summed[0],
        summed[1],
        grad_gates,
        grad_w_out,
    )


def solution(mesh):
    return jax.shard_map(
        per_device,
        mesh=mesh,
        in_specs=(
            P("seq", "head"),
            P("seq", "head"),
            P("seq", "head"),
            P("seq", "head"),
            P("seq"),
            P("head"),
            P("seq", "head"),
            P("head", None),
        ),
        out_specs=(
            P("seq", "head"),
            P("seq", "head"),
            P("seq", "head"),
            P("seq", "head"),
            P("head", "seq"),
        ),
        check_vma=False,
    )
```
